32 devices in a mesh: grp: 2 (over y), seq: 4 (over z), head: 4 (over x, core).
Axes of the slice: x: 2, y: 2, z: 4, core: 2. Of those that a mesh axis runs over, the one named last changes fastest.
Arguments:
- queries: bfloat16 [4096, 8, 512], P(('grp', 'seq'), 'head'), parts along dimension 0, may hold values from -30 to 30
- keys: bfloat16 [4096, 8, 128], P(('grp', 'seq'), 'head'), parts along dimension 0, may hold values from -30 to 30
- values: bfloat16 [4096, 8, 128], P(('grp', 'seq'), 'head'), parts along dimension 0, may hold values from -6 to 6
- doc_blocks: int32 [8], P('grp'), parts along dimension 0, may hold values from 1 to 8, 16 in all
Outputs:
- attended: bfloat16 [4096, 8, 512], P(('grp', 'seq'), 'head'), parts along dimension 0
The draws below stay inside these ranges and needn't reach their ends.
There are 2 independent parts, one for each index of `grp`. The reference program is written for one: setup_inputs(seed, part) draws one part's arguments, and reference() takes and returns one part's arrays. A program takes and returns all parts, laid end to end along the dimension named above; each array names one. Nothing has to cross between parts.
Inputs may be any that keep to these rules, and one draw needn't show every extreme that they name: `doc_blocks`: each document spans whole blocks; the longest has exactly 8 blocks and the lengths sum to 16.
All inputs are finite; a program needn't handle non-finite values.
Results may differ from the reference program's by a relative error of at most 0.0036.
Values may be sent and summed in bfloat16 or wider, within the bound.
No kernel may reach another device: no remote copies, remote signals or barrier semaphores. Data moves between devices by JAX's collectives and lax.ppermute only.
A program may use at most 64 MiB of HBM per device.

```python
import math
import jax
import jax.numpy as jnp
import numpy as np
from jax import lax

HD = 128
KVH = 8
QPK = 4
TOK_DEV = 512
BLK = 128
TOKENS = 2048
BLOCKS = 16
DOC_BLK = 8
DOCS = 4


def joint_draw(key):
    query_key = jax.random.fold_in(key, 101)
    key_key = jax.random.fold_in(key, 202)
    base_q = jax.random.normal(query_key, (TOKENS, KVH, QPK * HD), jnp.float32)
    base_k = jax.random.normal(key_key, (TOKENS, KVH, HD), jnp.float32)
    return (jnp.clip(base_q, -6.0, 6.0), jnp.clip(base_k, -6.0, 6.0))


def draw_queries(key, part):
    return joint_draw(key)[0].astype(jnp.bfloat16)


def draw_keys(key, part):
    return joint_draw(key)[1].astype(jnp.bfloat16)


def block_scale(own_key, dims, pieces, smallest, top_value):
    def one(position, parts):
        steps = jax.random.uniform(jax.random.fold_in(jax.random.fold_in(own_key, 6), position), (parts,), jnp.float32, smallest / len(pieces), top_value / len(pieces))
        return jnp.repeat(jnp.exp(steps), dims[position] // parts).reshape((-1,) + (1,) * (len(dims) - position - 1))

    gain = one(*pieces[0])
    for cut in pieces[1:]:
        gain = gain * one(*cut)
    return gain


def split_up(count, total, most, skew):
    portions = [(1 << 20) // math.isqrt(grade ** skew) + 1 for grade in range(2, count + 1)]
    rest, holding = total - most - (count - 1), [1] * (count - 1)
    while rest > 0:
        candidates = [i for i in range(count - 1) if holding[i] < most]
        whole, budget = sum([portions[i] for i in candidates]), rest
        for i in candidates:
            addition = min(most - holding[i], max(1, budget * portions[i] // whole), rest)
            holding[i] = holding[i] + addition
            rest = rest - addition
    return np.array([most] + holding)


def uneven_parts(rng, amount, total, reach, skew):
    if amount == 2:
        one = jax.random.randint(rng, (), max(1, total - reach), min(reach, total - 1) + 1)
        return jnp.stack([one, total - one])
    tallies = jnp.asarray(split_up(amount, total, reach, skew), jnp.int32)
    couples = (amount - 1) // 2
    source_of, taker = tallies[1:1 + 2 * couples:2], tallies[2:2 + 2 * couples:2]
    margin = jnp.minimum(source_of - 1, reach - taker)
    passed = jax.random.randint(jax.random.fold_in(rng, 1), (couples,), 0, 1 << 20) % (margin + 1)
    tallies = tallies.at[1:1 + 2 * couples:2].set(source_of - passed).at[2:2 + 2 * couples:2].set(taker + passed)
    return tallies[jax.random.permutation(jax.random.fold_in(rng, 2), amount)]


def gaussian(key, shape, deviation, bound, split=(), kind=jnp.bfloat16):
    result = jax.random.normal(key, shape, jnp.float32) * deviation
    if len(split) > 0:
        result = block_scale(key, shape, split, -0.22, 0.18) * result
    return jnp.clip(result, min=-bound, max=bound).astype(kind)


def setup_inputs(seed: int = 0, part: int = 0) -> dict:
    key_of = jax.random.split(jax.random.key(seed), 5)
    part_keys = jax.random.split(jax.random.fold_in(key_of[4], part), 5)
    return {
        "queries": draw_queries(jax.random.fold_in(jax.random.fold_in(key_of[4], part), 71), part),
        "keys": draw_keys(jax.random.fold_in(jax.random.fold_in(key_of[4], part), 71), part),
        "values": gaussian(part_keys[2], (TOKENS, KVH, HD), 1.0, 6.0, ((0, 4), (1, 4))),
        "doc_blocks": uneven_parts(part_keys[3], DOCS, BLOCKS, DOC_BLK, 2).astype(jnp.int32),
    }


def doc_ids(lengths, positions, block_size):
    doc_ends = jnp.cumsum(lengths).astype(jnp.int32)
    doc_starts = (doc_ends - lengths) * block_size
    return jnp.sum((positions[:, None] >= doc_starts[None, :]).astype(jnp.int32), axis=1) - 1


def window_attend(queries, key_window, value_window, query_doc, key_doc, query_block, reach_tokens, score_scale):
    row_count = queries.shape[0]
    head_count = queries.shape[1]
    head_dim = key_window.shape[-1]
    width = reach_tokens + query_block
    results = []
    for head in range(head_count):
        query_head = queries[:, head:head + 1]
        key_head = key_window[:, head:head + 1]
        value_head = value_window[:, head:head + 1]

        def one_block(block_index):
            offset = block_index * query_block
            query_rows = lax.dynamic_slice_in_dim(query_head, offset, query_block, 0)
            key_rows = lax.dynamic_slice_in_dim(key_head, offset, width, 0)
            value_rows = lax.dynamic_slice_in_dim(value_head, offset, width, 0)
            q_doc = lax.dynamic_slice_in_dim(query_doc, offset, query_block, 0)
            k_doc = lax.dynamic_slice_in_dim(key_doc, offset, width, 0)
            q_pos = offset + reach_tokens + jnp.arange(query_block, dtype=jnp.int32)
            k_pos = offset + jnp.arange(width, dtype=jnp.int32)
            grouped = query_rows.reshape(query_block, 1, -1, head_dim).astype(jnp.float32)
            scores = jnp.einsum("qhgd,khd->hgqk", grouped, key_rows.astype(jnp.float32)) * score_scale
            allowed = (k_doc[None, :] == q_doc[:, None]) & (k_pos[None, :] <= q_pos[:, None])
            scores = jnp.where(allowed[None, None], scores, -jnp.inf)
            row_max = jnp.max(scores, axis=-1)
            probability = jnp.exp(scores - row_max[..., None])
            row_sum = jnp.sum(probability, axis=-1)
            prob_b = probability.astype(jnp.bfloat16).astype(jnp.float32)
            weighted = jnp.einsum("hgqk,khd->qhgd", prob_b, value_rows.astype(jnp.float32))
            normed = weighted / jnp.transpose(row_sum, (2, 0, 1))[..., None]
            return normed.reshape(query_block, 1, -1).astype(jnp.bfloat16)

        blocks = lax.map(one_block, jnp.arange(row_count // query_block, dtype=jnp.int32))
        results.append(blocks.reshape(row_count, 1, -1))
    return jnp.concatenate(results, axis=1)


def reference(queries, keys, values, doc_blocks):
    reach_tokens = DOC_BLK * BLK
    query_block = min(128, TOK_DEV)
    positions = jnp.arange(TOKENS, dtype=jnp.int32)
    query_doc = doc_ids(doc_blocks, positions, BLK)
    key_doc = jnp.concatenate([jnp.full((reach_tokens,), -1, jnp.int32), query_doc])
    padding = jnp.zeros((reach_tokens, KVH, HD), keys.dtype)
    key_window = jnp.concatenate([padding, keys], axis=0)
    value_window = jnp.concatenate([padding, values], axis=0)
    return window_attend(queries, key_window, value_window, query_doc, key_doc, query_block, reach_tokens, HD ** -0.5)
```

```python
import jax
import jax.numpy as jnp
from jax import lax
from jax.experimental import pallas as pl
from jax.experimental.pallas import tpu as pltpu
from jax.sharding import PartitionSpec as P

BLK = 128


def shift_up(block, axis):
    size = lax.axis_size(axis)
    return lax.ppermute(block, axis, [(i, i + 1) for i in range(size - 1)])


def first_needed(distance, reach, dev_blocks):
    return max(0, (distance - reach) * dev_blocks + 1)


def make_kernel(dev_blocks, doc_blk, reach, firsts, groups, head_dim, score_scale):
    rows = groups * BLK
    slots = doc_blk

    def source_of(rel):
        if rel >= 0:
            return 0, rel
        distance = (-rel + dev_blocks - 1) // dev_blocks
        return distance, rel + distance * dev_blocks - firsts[distance]

    def kernel(rel_ref, q_ref, *refs):
        k_refs = refs[: reach + 1]
        v_refs = refs[reach + 1 : 2 * reach + 2]
        o_ref = refs[2 * reach + 2]
        s_sc, m_sc, l_sc, acc_sc = refs[2 * reach + 3 :]
        for i in range(dev_blocks):
            start = rel_ref[i]
            q = jnp.concatenate(
                [q_ref[i * BLK : (i + 1) * BLK, g * head_dim : (g + 1) * head_dim] for g in range(groups)],
                axis=0,
            )
            m_sc[...] = jnp.full(m_sc.shape, -jnp.inf, jnp.float32)
            l_sc[...] = jnp.zeros(l_sc.shape, jnp.float32)
            acc_sc[...] = jnp.zeros(acc_sc.shape, jnp.float32)
            cands = []
            for t in range(slots):
                rel = i - slots + 1 + t
                src, j = source_of(rel)
                if src > reach or j < 0:
                    continue
                cands.append((t, rel, src, j))

            for t, rel, src, j in cands:
                @pl.when(start <= rel)
                def _():
                    k = k_refs[src][j * BLK : (j + 1) * BLK, :]
                    s = lax.dot_general(
                        q, k, (((1,), (1,)), ((), ())), preferred_element_type=jnp.float32
                    ) * score_scale
                    if rel == i:
                        row = lax.broadcasted_iota(jnp.int32, s.shape, 0) % BLK
                        col = lax.broadcasted_iota(jnp.int32, s.shape, 1)
                        s = jnp.where(col <= row, s, -jnp.inf)
                    s_sc[t] = s
                    m_sc[...] = jnp.maximum(m_sc[...], s)

            row_max = jnp.max(m_sc[...], axis=1, keepdims=True)

            for t, rel, src, j in cands:
                @pl.when(start <= rel)
                def _():
                    p = jnp.exp(s_sc[t] - row_max)
                    l_sc[...] = l_sc[...] + p
                    v = v_refs[src][j * BLK : (j + 1) * BLK, :]
                    acc_sc[...] = acc_sc[...] + jnp.dot(
                        p.astype(jnp.bfloat16), v, preferred_element_type=jnp.float32
                    )

            row_sum = jnp.sum(l_sc[...], axis=1, keepdims=True)
            out = acc_sc[...] / row_sum
            for g in range(groups):
                o_ref[i * BLK : (i + 1) * BLK, g * head_dim : (g + 1) * head_dim] = out[
                    g * BLK : (g + 1) * BLK
                ].astype(o_ref.dtype)

    return kernel, rows


def doc_start_of(doc_blocks, blocks):
    ends = jnp.cumsum(doc_blocks)
    starts = ends - doc_blocks
    return jnp.max(jnp.where(starts[None, :] <= blocks[:, None], starts[None, :], 0), axis=1)


def on_device(queries, keys, values, doc_blocks):
    tok_rows, heads, qwidth = queries.shape
    head_dim = keys.shape[2]
    groups = qwidth // head_dim
    dev_blocks = tok_rows // BLK
    score_scale = head_dim ** (-0.5)
    reach = min(4, lax.axis_size("seq") // 2)
    doc_blk = reach * dev_blocks
    firsts = [0] + [first_needed(r, reach, dev_blocks) for r in range(1, reach + 1)]

    device_pos = lax.axis_index("seq")
    first_block = device_pos * dev_blocks
    q_blocks = first_block + jnp.arange(dev_blocks, dtype=jnp.int32)
    rel_start = (doc_start_of(doc_blocks, q_blocks) - first_block).astype(jnp.int32)

    q2 = queries.reshape(tok_rows, heads * qwidth)
    k2 = keys.reshape(tok_rows, heads * head_dim)
    v2 = values.reshape(tok_rows, heads * head_dim)

    k_src, v_src = [k2], [v2]
    k_cur, v_cur = k2, v2
    prev_first = 0
    for r in range(1, reach + 1):
        cut = (firsts[r] - prev_first) * BLK
        k_cur, v_cur = shift_up((k_cur[cut:], v_cur[cut:]), "seq")
        prev_first = firsts[r]
        k_src.append(k_cur)
        v_src.append(v_cur)

    kernel, rows = make_kernel(dev_blocks, doc_blk, reach, firsts, groups, head_dim, score_scale)
    kv_specs = [
        pl.BlockSpec((src.shape[0], head_dim), lambda h, rel: (0, h)) for src in k_src
    ]
    out = pl.pallas_call(
        kernel,
        out_shape=jax.ShapeDtypeStruct((tok_rows, heads * qwidth), queries.dtype),
        grid_spec=pltpu.PrefetchScalarGridSpec(
            num_scalar_prefetch=1,
            grid=(heads,),
            in_specs=[pl.BlockSpec((tok_rows, qwidth), lambda h, rel: (0, h))] + kv_specs + kv_specs,
            out_specs=pl.BlockSpec((tok_rows, qwidth), lambda h, rel: (0, h)),
            scratch_shapes=[
                pltpu.VMEM((doc_blk, rows, head_dim), jnp.float32),
                pltpu.VMEM((rows, head_dim), jnp.float32),
                pltpu.VMEM((rows, head_dim), jnp.float32),
                pltpu.VMEM((rows, head_dim), jnp.float32),
            ],
        ),
        compiler_params=pltpu.CompilerParams(dimension_semantics=("arbitrary",)),
    )(rel_start, q2, *k_src, *v_src)
    return out.reshape(tok_rows, heads, qwidth)


def solution(mesh):
    placed = (
        P(("grp", "seq"), "head", None),
        P(("grp", "seq"), "head", None),
        P(("grp", "seq"), "head", None),
        P("grp"),
    )
    return jax.shard_map(
        on_device,
        mesh=mesh,
        in_specs=placed,
        out_specs=P(("grp", "seq"), "head", None),
        check_vma=False,
    )
```

```python
import jax
import jax.numpy as jnp
from jax import lax
from jax.experimental import pallas as pl
from jax.experimental.pallas import tpu as pltpu
from jax.sharding import PartitionSpec as P


BLK = 128


def shift_up(block, axis):
    size = lax.axis_size(axis)
    return lax.ppermute(block, axis, [(i, i + 1) for i in range(size - 1)])


def first_needed(distance, reach, dev_blocks):
    return max(0, (distance - reach) * dev_blocks + 1)


def stage_regions(stage, i, dev_blocks, doc_blk, firsts):
    if stage == 0:
        lo, hi = 0, i
    else:
        lo = -stage * dev_blocks + firsts[stage]
        hi = -(stage - 1) * dev_blocks - 1
    lo = max(lo, i - doc_blk + 1)
    rels = list(range(lo, hi + 1))
    regions = []
    while rels:
        take = 2 if len(rels) % 2 == 0 else 1
        regions.append(rels[:take])
        rels = rels[take:]
    return regions


def make_stage(stage, first, last, dev_blocks, doc_blk, firsts, groups, head_dim, score_scale):
    def local_index(rel):
        if stage == 0:
            return rel
        return rel + stage * dev_blocks - firsts[stage]

    def kernel(rel_ref, q_ref, k_ref, v_ref, *refs):
        if first:
            acc_in = m_in = l_in = None
            rest = refs
        else:
            acc_in, m_in, l_in = refs[:3]
            rest = refs[3:]
        if last:
            o_ref = rest[0]
            s_sc, m_sc, l_sc, acc_sc = rest[1:]
        else:
            acc_out, m_out, l_out = rest[:3]
            s_sc, m_sc, l_sc, acc_sc = rest[3:]

        for i in range(dev_blocks):
            start = rel_ref[i]
            regions = stage_regions(stage, i, dev_blocks, doc_blk, firsts)
            if first:
                m_old = jnp.full((1, groups * BLK), -jnp.inf, jnp.float32)
                l_old = jnp.zeros((1, groups * BLK), jnp.float32)
            else:
                m_old = m_in[i : i + 1, :]
                l_old = l_in[i : i + 1, :]
            m_sc[...] = m_old
            if not regions:
                m_new = m_old
                l_sc[...] = l_old
                if first:
                    acc_sc[...] = jnp.zeros(acc_sc.shape, jnp.float32)
                else:
                    acc_sc[...] = acc_in[i]
            else:
                q = jnp.concatenate(
                    [q_ref[i * BLK : (i + 1) * BLK, g * head_dim : (g + 1) * head_dim] for g in range(groups)],
                    axis=0,
                )

                def scores(rels):
                    lo = local_index(rels[0])
                    k = k_ref[lo * BLK : (lo + len(rels)) * BLK, :]
                    s = lax.dot_general(
                        k, q, (((1,), (1,)), ((), ())), preferred_element_type=jnp.float32
                    ) * score_scale
                    if rels[-1] == i:
                        key = lax.broadcasted_iota(jnp.int32, s.shape, 0) + (rels[0] - i) * BLK
                        tok = lax.broadcasted_iota(jnp.int32, s.shape, 1) % BLK
                        s = jnp.where(key <= tok, s, -jnp.inf)
                    return s

                def variants(rels):
                    out = [(rels, start <= rels[0])]
                    if len(rels) == 2:
                        out.append((rels[1:], start == rels[1]))
                    return out

                for r, rels in enumerate(regions):
                    for sub, cond in variants(rels):
                        @pl.when(cond)
                        def _():
                            s = scores(sub)
                            s_sc[r, : len(sub) * BLK, :] = s
                            m_sc[...] = jnp.maximum(m_sc[...], jnp.max(s, axis=0, keepdims=True))

                m_new = m_sc[...]
                alpha = jnp.exp(m_old - m_new)
                l_sc[...] = alpha * l_old
                if first:
                    acc_sc[...] = jnp.zeros(acc_sc.shape, jnp.float32)
                else:
                    acc_sc[...] = alpha * acc_in[i]

                for r, rels in enumerate(regions):
                    for sub, cond in variants(rels):
                        @pl.when(cond)
                        def _():
                            p = jnp.exp(s_sc[r, : len(sub) * BLK, :] - m_new)
                            l_sc[...] = l_sc[...] + jnp.sum(p, axis=0, keepdims=True)
                            lo = local_index(sub[0])
                            v = v_ref[lo * BLK : (lo + len(sub)) * BLK, :]
                            acc_sc[...] = acc_sc[...] + lax.dot_general(
                                v, p.astype(jnp.bfloat16), (((0,), (0,)), ((), ())),
                                preferred_element_type=jnp.float32,
                            )

            if last:
                out_t = acc_sc[...] / l_sc[...]
                out = jnp.transpose(out_t)
                for g in range(groups):
                    o_ref[i * BLK : (i + 1) * BLK, g * head_dim : (g + 1) * head_dim] = out[
                        g * BLK : (g + 1) * BLK
                    ].astype(o_ref.dtype)
            else:
                acc_out[i] = acc_sc[...]
                m_out[i : i + 1, :] = m_new if regions else m_old
                l_out[i : i + 1, :] = l_sc[...]

    return kernel


def doc_start_of(doc_blocks, blocks):
    ends = jnp.cumsum(doc_blocks)
    starts = ends - doc_blocks
    return jnp.max(jnp.where(starts[None, :] <= blocks[:, None], starts[None, :], 0), axis=1)


def on_device(queries, keys, values, doc_blocks):
    tok_rows, heads, qwidth = queries.shape
    head_dim = keys.shape[2]
    groups = qwidth // head_dim
    rows = groups * BLK
    dev_blocks = tok_rows // BLK
    score_scale = head_dim ** (-0.5)
    reach = min(4, lax.axis_size("seq") // 2)
    doc_blk = reach * dev_blocks
    firsts = [0] + [first_needed(r, reach, dev_blocks) for r in range(1, reach + 1)]

    device_pos = lax.axis_index("seq")
    first_block = device_pos * dev_blocks
    q_blocks = first_block + jnp.arange(dev_blocks, dtype=jnp.int32)
    rel_start = (doc_start_of(doc_blocks, q_blocks) - first_block).astype(jnp.int32)

    q2 = queries.reshape(tok_rows, heads * qwidth)
    k2 = keys.reshape(tok_rows, heads * head_dim)
    v2 = values.reshape(tok_rows, heads * head_dim)

    k_src, v_src = [k2], [v2]
    k_cur, v_cur = k2, v2
    prev_first = 0
    for r in range(1, reach + 1):
        cut = (firsts[r] - prev_first) * BLK
        k_cur, v_cur = shift_up((k_cur[cut:], v_cur[cut:]), "seq")
        prev_first = firsts[r]
        k_src.append(k_cur)
        v_src.append(v_cur)

    state_shapes = (
        jax.ShapeDtypeStruct((heads, dev_blocks, head_dim, rows), jnp.float32),
        jax.ShapeDtypeStruct((heads, dev_blocks, rows), jnp.float32),
        jax.ShapeDtypeStruct((heads, dev_blocks, rows), jnp.float32),
    )
    state_specs = [
        pl.BlockSpec((None, dev_blocks, head_dim, rows), lambda h, rel: (h, 0, 0, 0)),
        pl.BlockSpec((None, dev_blocks, rows), lambda h, rel: (h, 0, 0)),
        pl.BlockSpec((None, dev_blocks, rows), lambda h, rel: (h, 0, 0)),
    ]
    scratch = [
        pltpu.VMEM((max(1, (dev_blocks + 1) // 2), 2 * BLK, rows), jnp.float32),
        pltpu.VMEM((1, rows), jnp.float32),
        pltpu.VMEM((1, rows), jnp.float32),
        pltpu.VMEM((head_dim, rows), jnp.float32),
    ]
    q_spec = pl.BlockSpec((tok_rows, qwidth), lambda h, rel: (0, h))

    state = None
    out = None
    for stage in range(reach + 1):
        first = stage == 0
        last = stage == reach
        kernel = make_stage(stage, first, last, dev_blocks, doc_blk, firsts, groups, head_dim, score_scale)
        kv_spec = pl.BlockSpec((k_src[stage].shape[0], head_dim), lambda h, rel: (0, h))
        in_specs = [q_spec, kv_spec, kv_spec] + ([] if first else state_specs)
        args = [rel_start, q2, k_src[stage], v_src[stage]] + ([] if first else list(state))
        if last:
            out_shape = jax.ShapeDtypeStruct((tok_rows, heads * qwidth), queries.dtype)
            out_specs = q_spec
        else:
            out_shape = state_shapes
            out_specs = state_specs
        res = pl.pallas_call(
            kernel,
            out_shape=out_shape,
            grid_spec=pltpu.PrefetchScalarGridSpec(
                num_scalar_prefetch=1,
                grid=(heads,),
                in_specs=in_specs,
                out_specs=out_specs,
                scratch_shapes=scratch,
            ),
            compiler_params=pltpu.CompilerParams(dimension_semantics=("arbitrary",)),
        )(*args)
        if last:
            out = res
        else:
            state = res
    return out.reshape(tok_rows, heads, qwidth)


def solution(mesh):
    placed = (
        P(("grp", "seq"), "head", None),
        P(("grp", "seq"), "head", None),
        P(("grp", "seq"), "head", None),
        P("grp"),
    )

    return jax.shard_map(
        on_device,
        mesh=mesh,
        in_specs=placed,
        out_specs=P(("grp", "seq"), "head", None),
        check_vma=False,
    )
```

```python
import jax
import jax.numpy as jnp
from jax import lax
from jax.experimental import pallas as pl
from jax.experimental.pallas import tpu as pltpu
from jax.sharding import PartitionSpec as P


BLK = 128


def shift_up(block, axis):
    size = lax.axis_size(axis)
    return lax.ppermute(block, axis, [(i, i + 1) for i in range(size - 1)])


def first_needed(distance, reach, dev_blocks):
    return max(0, (distance - reach) * dev_blocks + 1)


def stage_regions(stage, i, dev_blocks, doc_blk, firsts):
    if stage == 0:
        lo, hi = 0, i
    else:
        lo = -stage * dev_blocks + firsts[stage]
        hi = -(stage - 1) * dev_blocks - 1
    lo = max(lo, i - doc_blk + 1)
    rels = list(range(lo, hi + 1))
    regions = []
    while rels:
        take = 2 if len(rels) % 2 == 0 else 1
        regions.append(rels[:take])
        rels = rels[take:]
    return regions


def make_stage(stage, first, last, dev_blocks, doc_blk, firsts, groups, head_dim, score_scale):
    def local_index(rel):
        if stage == 0:
            return rel
        return rel + stage * dev_blocks - firsts[stage]

    def kernel(rel_ref, q_ref, kv_ref, *refs):
        k_ref = kv_ref.at[0]
        v_ref = kv_ref.at[1]
        if first:
            acc_in = m_in = l_in = None
            rest = refs
        else:
            acc_in, m_in, l_in = refs[:3]
            rest = refs[3:]
        if last:
            o_ref = rest[0]
            s_sc, m_sc, l_sc, acc_sc = rest[1:]
        else:
            acc_out, m_out, l_out = rest[:3]
            s_sc, m_sc, l_sc, acc_sc = rest[3:]

        for i in range(dev_blocks):
            start = rel_ref[i]
            regions = stage_regions(stage, i, dev_blocks, doc_blk, firsts)
            if first:
                m_old = jnp.full((1, groups * BLK), -jnp.inf, jnp.float32)
                l_old = jnp.zeros((1, groups * BLK), jnp.float32)
            else:
                m_old = m_in[i : i + 1, :]
                l_old = l_in[i : i + 1, :]
            m_sc[...] = m_old
            if not regions:
                m_new = m_old
                l_sc[...] = l_old
                if first:
                    acc_sc[...] = jnp.zeros(acc_sc.shape, jnp.float32)
                else:
                    acc_sc[...] = acc_in[i]
            else:
                q = jnp.concatenate(
                    [q_ref[i * BLK : (i + 1) * BLK, g * head_dim : (g + 1) * head_dim] for g in range(groups)],
                    axis=0,
                )

                def scores(rels):
                    lo = local_index(rels[0])
                    k = k_ref[lo * BLK : (lo + len(rels)) * BLK, :]
                    s = lax.dot_general(
                        k, q, (((1,), (1,)), ((), ())), preferred_element_type=jnp.float32
                    ) * score_scale
                    if rels[-1] == i:
                        key = lax.broadcasted_iota(jnp.int32, s.shape, 0) + (rels[0] - i) * BLK
                        tok = lax.broadcasted_iota(jnp.int32, s.shape, 1) % BLK
                        s = jnp.where(key <= tok, s, -jnp.inf)
                    return s

                def variants(rels):
                    out = [(rels, start <= rels[0])]
                    if len(rels) == 2:
                        out.append((rels[1:], start == rels[1]))
                    return out

                for r, rels in enumerate(regions):
                    for sub, cond in variants(rels):
                        @pl.when(cond)
                        def _():
                            s = scores(sub)
                            s_sc[r, : len(sub) * BLK, :] = s
                            m_sc[...] = jnp.maximum(m_sc[...], jnp.max(s, axis=0, keepdims=True))

                m_new = m_sc[...]
                alpha = jnp.exp(m_old - m_new)
                l_sc[...] = alpha * l_old
                if first:
                    acc_sc[...] = jnp.zeros(acc_sc.shape, jnp.float32)
                else:
                    acc_sc[...] = alpha * acc_in[i]

                for r, rels in enumerate(regions):
                    for sub, cond in variants(rels):
                        @pl.when(cond)
                        def _():
                            p = jnp.exp(s_sc[r, : len(sub) * BLK, :] - m_new)
                            l_sc[...] = l_sc[...] + jnp.sum(p, axis=0, keepdims=True)
                            lo = local_index(sub[0])
                            v = v_ref[lo * BLK : (lo + len(sub)) * BLK, :]
                            acc_sc[...] = acc_sc[...] + lax.dot_general(
                                v, p.astype(jnp.bfloat16), (((0,), (0,)), ((), ())),
                                preferred_element_type=jnp.float32,
                            )

            if last:
                out_t = acc_sc[...] / l_sc[...]
                out = jnp.transpose(out_t)
                for g in range(groups):
                    o_ref[i * BLK : (i + 1) * BLK, g * head_dim : (g + 1) * head_dim] = out[
                        g * BLK : (g + 1) * BLK
                    ].astype(o_ref.dtype)
            else:
                acc_out[i] = acc_sc[...]
                m_out[i : i + 1, :] = m_new if regions else m_old
                l_out[i : i + 1, :] = l_sc[...]

    return kernel


def doc_start_of(doc_blocks, blocks):
    ends = jnp.cumsum(doc_blocks)
    starts = ends - doc_blocks
    return jnp.max(jnp.where(starts[None, :] <= blocks[:, None], starts[None, :], 0), axis=1)


def on_device(queries, keys, values, doc_blocks):
    tok_rows, heads, qwidth = queries.shape
    head_dim = keys.shape[2]
    groups = qwidth // head_dim
    rows = groups * BLK
    dev_blocks = tok_rows // BLK
    score_scale = head_dim ** (-0.5)
    reach = min(4, lax.axis_size("seq") // 2)
    doc_blk = reach * dev_blocks
    firsts = [0] + [first_needed(r, reach, dev_blocks) for r in range(1, reach + 1)]

    device_pos = lax.axis_index("seq")
    first_block = device_pos * dev_blocks
    q_blocks = first_block + jnp.arange(dev_blocks, dtype=jnp.int32)
    rel_start = (doc_start_of(doc_blocks, q_blocks) - first_block).astype(jnp.int32)

    q2 = queries.reshape(tok_rows, heads * qwidth)
    k2 = keys.reshape(tok_rows, heads * head_dim)
    v2 = values.reshape(tok_rows, heads * head_dim)

    kv_cur = jnp.stack([k2, v2])
    kv_src = [kv_cur]
    prev_first = 0
    for r in range(1, reach + 1):
        cut = (firsts[r] - prev_first) * BLK
        kv_cur = shift_up(kv_cur[:, cut:], "seq")
        prev_first = firsts[r]
        kv_src.append(kv_cur)

    state_shapes = (
        jax.ShapeDtypeStruct((heads, dev_blocks, head_dim, rows), jnp.float32),
        jax.ShapeDtypeStruct((heads, dev_blocks, rows), jnp.float32),
        jax.ShapeDtypeStruct((heads, dev_blocks, rows), jnp.float32),
    )
    state_specs = [
        pl.BlockSpec((None, dev_blocks, head_dim, rows), lambda h, rel: (h, 0, 0, 0)),
        pl.BlockSpec((None, dev_blocks, rows), lambda h, rel: (h, 0, 0)),
        pl.BlockSpec((None, dev_blocks, rows), lambda h, rel: (h, 0, 0)),
    ]
    scratch = [
        pltpu.VMEM((max(1, (dev_blocks + 1) // 2), 2 * BLK, rows), jnp.float32),
        pltpu.VMEM((1, rows), jnp.float32),
        pltpu.VMEM((1, rows), jnp.float32),
        pltpu.VMEM((head_dim, rows), jnp.float32),
    ]
    q_spec = pl.BlockSpec((tok_rows, qwidth), lambda h, rel: (0, h))

    state = None
    out = None
    for stage in range(reach + 1):
        first = stage == 0
        last = stage == reach
        kernel = make_stage(stage, first, last, dev_blocks, doc_blk, firsts, groups, head_dim, score_scale)
        kv_spec = pl.BlockSpec((2, kv_src[stage].shape[1], head_dim), lambda h, rel: (0, 0, h))
        in_specs = [q_spec, kv_spec] + ([] if first else state_specs)
        args = [rel_start, q2, kv_src[stage]] + ([] if first else list(state))
        if last:
            out_shape = jax.ShapeDtypeStruct((tok_rows, heads * qwidth), queries.dtype)
            out_specs = q_spec
        else:
            out_shape = state_shapes
            out_specs = state_specs
        res = pl.pallas_call(
            kernel,
            out_shape=out_shape,
            grid_spec=pltpu.PrefetchScalarGridSpec(
                num_scalar_prefetch=1,
                grid=(heads,),
                in_specs=in_specs,
                out_specs=out_specs,
                scratch_shapes=scratch,
            ),
            compiler_params=pltpu.CompilerParams(dimension_semantics=("arbitrary",)),
        )(*args)
        if last:
            out = res
        else:
            state = res
    return out.reshape(tok_rows, heads, qwidth)


def solution(mesh):
    placed = (
        P(("grp", "seq"), "head", None),
        P(("grp", "seq"), "head", None),
        P(("grp", "seq"), "head", None),
        P("grp"),
    )

    return jax.shard_map(
        on_device,
        mesh=mesh,
        in_specs=placed,
        out_specs=P(("grp", "seq"), "head", None),
        check_vma=False,
    )
```

```python
import jax
import jax.numpy as jnp
from jax import lax
from jax.experimental import pallas as pl
from jax.experimental.pallas import tpu as pltpu
from jax.sharding import PartitionSpec as P


BLK = 128


def shift_up(block, axis):
    size = lax.axis_size(axis)
    return lax.ppermute(block, axis, [(i, i + 1) for i in range(size - 1)])


def first_needed(distance, reach, dev_blocks):
    return max(0, (distance - reach) * dev_blocks + 1)


def stage_regions(stage, i, dev_blocks, doc_blk, firsts):
    if stage == 0:
        lo, hi = 0, i
    else:
        lo = -stage * dev_blocks + firsts[stage]
        hi = -(stage - 1) * dev_blocks - 1
    lo = max(lo, i - doc_blk + 1)
    rels = list(range(lo, hi + 1))
    regions = []
    while rels:
        take = 2 if len(rels) % 2 == 0 else 1
        regions.append(rels[:take])
        rels = rels[take:]
    return regions


def make_stage(stage, first, last, dev_blocks, doc_blk, firsts, groups, head_dim, score_scale):
    def local_index(rel):
        if stage == 0:
            return rel
        return rel + stage * dev_blocks - firsts[stage]

    def kernel(rel_ref, q_ref, kv_ref, *refs):
        k_ref = kv_ref.at[0]
        v_ref = kv_ref.at[1]
        if first:
            acc_in = m_in = l_in = None
            rest = refs
        else:
            acc_in, m_in, l_in = refs[:3]
            rest = refs[3:]
        if last:
            o_ref = rest[0]
            (s_sc,) = rest[1:]
        else:
            acc_out, m_out, l_out = rest[:3]
            (s_sc,) = rest[3:]

        for i in range(dev_blocks):
            start = rel_ref[i]
            regions = stage_regions(stage, i, dev_blocks, doc_blk, firsts)

            def finish(m_new, row_sum, acc):
                if last:
                    out = jnp.transpose(acc * (1.0 / row_sum))
                    for g in range(groups):
                        o_ref[i * BLK : (i + 1) * BLK, g * head_dim : (g + 1) * head_dim] = out[
                            g * BLK : (g + 1) * BLK
                        ].astype(o_ref.dtype)
                else:
                    acc_out[i] = acc
                    m_out[i : i + 1, :] = m_new
                    l_out[i : i + 1, :] = row_sum

            def passthrough():
                finish(m_in[i : i + 1, :], l_in[i : i + 1, :], acc_in[i])

            if not regions:
                passthrough()
                continue

            def compute():
                q = jnp.concatenate(
                    [q_ref[i * BLK : (i + 1) * BLK, g * head_dim : (g + 1) * head_dim] for g in range(groups)],
                    axis=0,
                )
                m_blk = None
                for r, rels in enumerate(regions):
                    lo = local_index(rels[0])
                    k = k_ref[lo * BLK : (lo + len(rels)) * BLK, :]
                    sc = lax.dot_general(
                        k, q, (((1,), (1,)), ((), ())), preferred_element_type=jnp.float32
                    ) * score_scale
                    key = lax.broadcasted_iota(jnp.int32, sc.shape, 0) // BLK + rels[0]
                    keep = key >= start
                    if rels[-1] == i:
                        key_pos = lax.broadcasted_iota(jnp.int32, sc.shape, 0) + (rels[0] - i) * BLK
                        tok = lax.broadcasted_iota(jnp.int32, sc.shape, 1) % BLK
                        keep = keep & (key_pos <= tok)
                    sc = jnp.where(keep, sc, -jnp.inf)
                    s_sc[r, : len(rels) * BLK, :] = sc
                    mx = jnp.max(sc, axis=0, keepdims=True)
                    m_blk = mx if m_blk is None else jnp.maximum(m_blk, mx)
                if first:
                    m_new = m_blk
                    row_sum = jnp.zeros(m_new.shape, jnp.float32)
                    acc = jnp.zeros((head_dim, groups * BLK), jnp.float32)
                else:
                    m_old = m_in[i : i + 1, :]
                    m_new = jnp.maximum(m_old, m_blk)
                    alpha = jnp.exp(m_old - m_new)
                    row_sum = alpha * l_in[i : i + 1, :]
                    acc = alpha * acc_in[i]
                for r, rels in enumerate(regions):
                    p = jnp.exp(s_sc[r, : len(rels) * BLK, :] - m_new)
                    row_sum = row_sum + jnp.sum(p, axis=0, keepdims=True)
                    lo = local_index(rels[0])
                    v = v_ref[lo * BLK : (lo + len(rels)) * BLK, :]
                    acc = acc + lax.dot_general(
                        v, p.astype(jnp.bfloat16), (((0,), (0,)), ((), ())),
                        preferred_element_type=jnp.float32,
                    )
                finish(m_new, row_sum, acc)

            if first:
                compute()
            else:
                live = start <= regions[-1][-1]
                pl.when(live)(compute)
                pl.when(jnp.logical_not(live))(passthrough)

    return kernel


def doc_start_of(doc_blocks, blocks):
    ends = jnp.cumsum(doc_blocks)
    starts = ends - doc_blocks
    return jnp.max(jnp.where(starts[None, :] <= blocks[:, None], starts[None, :], 0), axis=1)


def on_device(queries, keys, values, doc_blocks):
    tok_rows, heads, qwidth = queries.shape
    head_dim = keys.shape[2]
    groups = qwidth // head_dim
    rows = groups * BLK
    dev_blocks = tok_rows // BLK
    score_scale = head_dim ** (-0.5)
    reach = min(4, lax.axis_size("seq") // 2)
    doc_blk = reach * dev_blocks
    firsts = [0] + [first_needed(r, reach, dev_blocks) for r in range(1, reach + 1)]

    device_pos = lax.axis_index("seq")
    first_block = device_pos * dev_blocks
    q_blocks = first_block + jnp.arange(dev_blocks, dtype=jnp.int32)
    rel_start = (doc_start_of(doc_blocks, q_blocks) - first_block).astype(jnp.int32)

    q2 = queries.reshape(tok_rows, heads * qwidth)
    k2 = keys.reshape(tok_rows, heads * head_dim)
    v2 = values.reshape(tok_rows, heads * head_dim)

    kv_cur = jnp.stack([k2, v2])
    kv_src = [kv_cur]
    prev_first = 0
    for r in range(1, reach + 1):
        cut = (firsts[r] - prev_first) * BLK
        kv_cur = shift_up(kv_cur[:, cut:], "seq")
        prev_first = firsts[r]
        kv_src.append(kv_cur)

    state_shapes = (
        jax.ShapeDtypeStruct((heads, dev_blocks, head_dim, rows), jnp.float32),
        jax.ShapeDtypeStruct((heads, dev_blocks, rows), jnp.float32),
        jax.ShapeDtypeStruct((heads, dev_blocks, rows), jnp.float32),
    )
    state_specs = [
        pl.BlockSpec((None, dev_blocks, head_dim, rows), lambda h, rel: (h, 0, 0, 0)),
        pl.BlockSpec((None, dev_blocks, rows), lambda h, rel: (h, 0, 0)),
        pl.BlockSpec((None, dev_blocks, rows), lambda h, rel: (h, 0, 0)),
    ]
    scratch = [
        pltpu.VMEM((max(1, (dev_blocks + 1) // 2), 2 * BLK, rows), jnp.float32),
    ]
    q_spec = pl.BlockSpec((tok_rows, qwidth), lambda h, rel: (0, h))

    state = None
    out = None
    for stage in range(reach + 1):
        first = stage == 0
        last = stage == reach
        kernel = make_stage(stage, first, last, dev_blocks, doc_blk, firsts, groups, head_dim, score_scale)
        kv_spec = pl.BlockSpec((2, kv_src[stage].shape[1], head_dim), lambda h, rel: (0, 0, h))
        in_specs = [q_spec, kv_spec] + ([] if first else state_specs)
        args = [rel_start, q2, kv_src[stage]] + ([] if first else list(state))
        if last:
            out_shape = jax.ShapeDtypeStruct((tok_rows, heads * qwidth), queries.dtype)
            out_specs = q_spec
        else:
            out_shape = state_shapes
            out_specs = state_specs
        res = pl.pallas_call(
            kernel,
            out_shape=out_shape,
            grid_spec=pltpu.PrefetchScalarGridSpec(
                num_scalar_prefetch=1,
                grid=(heads,),
                in_specs=in_specs,
                out_specs=out_specs,
                scratch_shapes=scratch,
            ),
            compiler_params=pltpu.CompilerParams(dimension_semantics=("arbitrary",)),
        )(*args)
        if last:
            out = res
        else:
            state = res
    return out.reshape(tok_rows, heads, qwidth)


def solution(mesh):
    placed = (
        P(("grp", "seq"), "head", None),
        P(("grp", "seq"), "head", None),
        P(("grp", "seq"), "head", None),
        P("grp"),
    )

    return jax.shard_map(
        on_device,
        mesh=mesh,
        in_specs=placed,
        out_specs=P(("grp", "seq"), "head", None),
        check_vma=False,
    )
```

```python
import jax
import jax.numpy as jnp
from jax import lax
from jax.experimental import pallas as pl
from jax.experimental.pallas import tpu as pltpu
from jax.sharding import PartitionSpec as P


BLK = 128


def shift_up(block, axis):
    size = lax.axis_size(axis)
    return lax.ppermute(block, axis, [(i, i + 1) for i in range(size - 1)])


def first_needed(distance, reach, dev_blocks):
    return max(0, (distance - reach) * dev_blocks + 1)


def stage_regions(stage, i, dev_blocks, doc_blk, firsts):
    if stage == 0:
        lo, hi = 0, i
    else:
        lo = -stage * dev_blocks + firsts[stage]
        hi = -(stage - 1) * dev_blocks - 1
    lo = max(lo, i - doc_blk + 1)
    rels = list(range(lo, hi + 1))
    regions = []
    while rels:
        take = 2 if len(rels) % 2 == 0 else 1
        regions.append(rels[:take])
        rels = rels[take:]
    return regions


def make_stage(stage, first, last, dev_blocks, doc_blk, firsts, groups, head_dim, score_scale):
    def local_index(rel):
        if stage == 0:
            return rel
        return rel + stage * dev_blocks - firsts[stage]

    def kernel(rel_ref, q_ref, kv_ref, *refs):
        k_ref = kv_ref.at[0]
        v_ref = kv_ref.at[1]
        if first:
            acc_in = m_in = l_in = None
            rest = refs
        else:
            acc_in, m_in, l_in = refs[:3]
            rest = refs[3:]
        if last:
            o_ref = rest[0]
            (s_sc,) = rest[1:]
        else:
            acc_out, m_out, l_out = rest[:3]
            (s_sc,) = rest[3:]

        for i in range(dev_blocks):
            start = rel_ref[i]
            regions = stage_regions(stage, i, dev_blocks, doc_blk, firsts)

            def finish(m_new, row_sum, acc):
                if last:
                    out = jnp.transpose(acc * (1.0 / row_sum))
                    for g in range(groups):
                        o_ref[i * BLK : (i + 1) * BLK, g * head_dim : (g + 1) * head_dim] = out[
                            g * BLK : (g + 1) * BLK
                        ].astype(o_ref.dtype)
                else:
                    acc_out[i] = acc
                    m_out[i : i + 1, :] = m_new
                    l_out[i : i + 1, :] = row_sum

            def passthrough():
                finish(m_in[i : i + 1, :], l_in[i : i + 1, :], acc_in[i])

            if not regions:
                passthrough()
                continue

            def compute():
                q = jnp.concatenate(
                    [q_ref[i * BLK : (i + 1) * BLK, g * head_dim : (g + 1) * head_dim] for g in range(groups)],
                    axis=0,
                )
                m_blk = None
                for r, rels in enumerate(regions):
                    lo = local_index(rels[0])
                    k = k_ref[lo * BLK : (lo + len(rels)) * BLK, :]
                    sc = lax.dot_general(
                        k, q, (((1,), (1,)), ((), ())), preferred_element_type=jnp.float32
                    ) * score_scale
                    key = lax.broadcasted_iota(jnp.int32, sc.shape, 0) // BLK + rels[0]
                    keep = key >= start
                    if rels[-1] == i:
                        key_pos = lax.broadcasted_iota(jnp.int32, sc.shape, 0) + (rels[0] - i) * BLK
                        tok = lax.broadcasted_iota(jnp.int32, sc.shape, 1) % BLK
                        keep = keep & (key_pos <= tok)
                    sc = jnp.where(keep, sc, -jnp.inf)
                    s_sc[r, : len(rels) * BLK, :] = sc
                    mx = jnp.max(sc, axis=0, keepdims=True)
                    m_blk = mx if m_blk is None else jnp.maximum(m_blk, mx)
                if first:
                    m_new = m_blk
                    row_sum = jnp.zeros(m_new.shape, jnp.float32)
                    acc = jnp.zeros((head_dim, groups * BLK), jnp.float32)
                else:
                    m_old = m_in[i : i + 1, :]
                    m_new = jnp.maximum(m_old, m_blk)
                    alpha = jnp.exp(m_old - m_new)
                    row_sum = alpha * l_in[i : i + 1, :]
                    acc = alpha * acc_in[i]
                for r, rels in enumerate(regions):
                    p = jnp.exp(s_sc[r, : len(rels) * BLK, :] - m_new)
                    row_sum = row_sum + jnp.sum(p, axis=0, keepdims=True)
                    lo = local_index(rels[0])
                    v = v_ref[lo * BLK : (lo + len(rels)) * BLK, :]
                    acc = acc + lax.dot_general(
                        v, p.astype(jnp.bfloat16), (((0,), (0,)), ((), ())),
                        preferred_element_type=jnp.float32,
                    )
                finish(m_new, row_sum, acc)

            if first:
                compute()
            else:
                live = start <= regions[-1][-1]
                pl.when(live)(compute)
                pl.when(jnp.logical_not(live))(passthrough)

    return kernel


def doc_start_of(doc_blocks, blocks):
    ends = jnp.cumsum(doc_blocks)
    starts = ends - doc_blocks
    return jnp.max(jnp.where(starts[None, :] <= blocks[:, None], starts[None, :], 0), axis=1)


def on_device(queries, keys, values, doc_blocks):
    tok_rows, heads, qwidth = queries.shape
    head_dim = keys.shape[2]
    groups = qwidth // head_dim
    rows = groups * BLK
    dev_blocks = tok_rows // BLK
    score_scale = head_dim ** (-0.5)
    reach = min(4, lax.axis_size("seq") // 2)
    doc_blk = reach * dev_blocks
    firsts = [0] + [first_needed(r, reach, dev_blocks) for r in range(1, reach + 1)]

    device_pos = lax.axis_index("seq")
    first_block = device_pos * dev_blocks
    q_blocks = first_block + jnp.arange(dev_blocks, dtype=jnp.int32)
    rel_start = (doc_start_of(doc_blocks, q_blocks) - first_block).astype(jnp.int32)

    q2 = queries.reshape(tok_rows, heads * qwidth)
    k2 = keys.reshape(tok_rows, heads * head_dim)
    v2 = values.reshape(tok_rows, heads * head_dim)

    kv_cur = jnp.stack([keys, values])
    kv_src = [jnp.stack([k2, v2])]
    prev_first = 0
    for r in range(1, reach + 1):
        cut = (firsts[r] - prev_first) * BLK
        kv_cur = shift_up(kv_cur[:, cut:], "seq")
        prev_first = firsts[r]
        kv_src.append(kv_cur.reshape(2, kv_cur.shape[1], heads * head_dim))

    state_shapes = (
        jax.ShapeDtypeStruct((heads, dev_blocks, head_dim, rows), jnp.float32),
        jax.ShapeDtypeStruct((heads, dev_blocks, rows), jnp.float32),
        jax.ShapeDtypeStruct((heads, dev_blocks, rows), jnp.float32),
    )
    state_specs = [
        pl.BlockSpec((None, dev_blocks, head_dim, rows), lambda h, rel: (h, 0, 0, 0)),
        pl.BlockSpec((None, dev_blocks, rows), lambda h, rel: (h, 0, 0)),
        pl.BlockSpec((None, dev_blocks, rows), lambda h, rel: (h, 0, 0)),
    ]
    scratch = [
        pltpu.VMEM((max(1, (dev_blocks + 1) // 2), 2 * BLK, rows), jnp.float32),
    ]
    q_spec = pl.BlockSpec((tok_rows, qwidth), lambda h, rel: (0, h))

    state = None
    out = None
    for stage in range(reach + 1):
        first = stage == 0
        last = stage == reach
        kernel = make_stage(stage, first, last, dev_blocks, doc_blk, firsts, groups, head_dim, score_scale)
        kv_spec = pl.BlockSpec((2, kv_src[stage].shape[1], head_dim), lambda h, rel: (0, 0, h))
        in_specs = [q_spec, kv_spec] + ([] if first else state_specs)
        args = [rel_start, q2, kv_src[stage]] + ([] if first else list(state))
        if last:
            out_shape = jax.ShapeDtypeStruct((tok_rows, heads * qwidth), queries.dtype)
            out_specs = q_spec
        else:
            out_shape = state_shapes
            out_specs = state_specs
        res = pl.pallas_call(
            kernel,
            out_shape=out_shape,
            grid_spec=pltpu.PrefetchScalarGridSpec(
                num_scalar_prefetch=1,
                grid=(heads,),
                in_specs=in_specs,
                out_specs=out_specs,
                scratch_shapes=scratch,
            ),
            compiler_params=pltpu.CompilerParams(dimension_semantics=("arbitrary",)),
        )(*args)
        if last:
            out = res
        else:
            state = res
    return out.reshape(tok_rows, heads, qwidth)


def solution(mesh):
    placed = (
        P(("grp", "seq"), "head", None),
        P(("grp", "seq"), "head", None),
        P(("grp", "seq"), "head", None),
        P("grp"),
    )

    return jax.shard_map(
        on_device,
        mesh=mesh,
        in_specs=placed,
        out_specs=P(("grp", "seq"), "head", None),
        check_vma=False,
    )
```

```python
import jax
import jax.numpy as jnp
from jax import lax
from jax.experimental import pallas as pl
from jax.experimental.pallas import tpu as pltpu
from jax.sharding import PartitionSpec as P


BLK = 128


def shift_up(block, axis):
    size = lax.axis_size(axis)
    return lax.ppermute(block, axis, [(i, i + 1) for i in range(size - 1)])


def first_needed(distance, reach, dev_blocks):
    return max(0, (distance - reach) * dev_blocks + 1)


def stage_regions(stage, i, dev_blocks, doc_blk, firsts):
    if stage == 0:
        lo, hi = 0, i
    else:
        lo = -stage * dev_blocks + firsts[stage]
        hi = -(stage - 1) * dev_blocks - 1
    lo = max(lo, i - doc_blk + 1)
    rels = list(range(lo, hi + 1))
    regions = []
    while rels:
        take = 2 if len(rels) % 2 == 0 else 1
        regions.append(rels[:take])
        rels = rels[take:]
    return regions


def make_stage(stage, first, last, heads, dev_blocks, doc_blk, firsts, groups, head_dim, score_scale):
    def local_index(rel):
        if stage == 0:
            return rel
        return rel + stage * dev_blocks - firsts[stage]

    def kernel(rel_ref, q_all, kv_all, *refs):
        if first:
            acc_in = m_in = l_in = None
            rest = refs
        else:
            acc_in, m_in, l_in = refs[:3]
            rest = refs[3:]
        o_sc = None
        if last:
            o_ref = rest[0]
            s_sc, o_sc = rest[1:]
        else:
            acc_out, m_out, l_out = rest[:3]
            (s_sc,) = rest[3:]
        for hh in range(heads):
            head_body(hh, rel_ref, q_all, kv_all, acc_in, m_in, l_in,
                      None if last else acc_out, None if last else m_out, None if last else l_out,
                      s_sc, o_sc)
        if last:
            for i in range(dev_blocks):
                for g in range(groups):
                    vals = jnp.stack([o_sc[hh, i, g * BLK : (g + 1) * BLK, :] for hh in range(heads)], axis=1)
                    o_ref[i * BLK : (i + 1) * BLK, :, g * head_dim : (g + 1) * head_dim] = vals.astype(o_ref.dtype)

    def head_body(hh, rel_ref, q_all, kv_all, acc_in_all, m_in_all, l_in_all, acc_out_all, m_out_all, l_out_all, s_sc, o_sc):
        q_ref = q_all.at[:, hh * groups * head_dim : (hh + 1) * groups * head_dim]
        k_ref = kv_all.at[0, :, hh * head_dim : (hh + 1) * head_dim]
        v_ref = kv_all.at[1, :, hh * head_dim : (hh + 1) * head_dim]
        acc_in = None if first else acc_in_all.at[hh]
        m_in = None if first else m_in_all.at[hh]
        l_in = None if first else l_in_all.at[hh]
        acc_out = None if last else acc_out_all.at[hh]
        m_out = None if last else m_out_all.at[hh]
        l_out = None if last else l_out_all.at[hh]

        for i in range(dev_blocks):
            start = rel_ref[i]
            regions = stage_regions(stage, i, dev_blocks, doc_blk, firsts)

            def finish(m_new, row_sum, acc):
                if last:
                    o_sc[hh, i] = jnp.transpose(acc * (1.0 / row_sum))
                else:
                    acc_out[i] = acc
                    m_out[i : i + 1, :] = m_new
                    l_out[i : i + 1, :] = row_sum

            def passthrough():
                finish(m_in[i : i + 1, :], l_in[i : i + 1, :], acc_in[i])

            if not regions:
                passthrough()
                continue

            def compute():
                q = jnp.concatenate(
                    [q_ref[i * BLK : (i + 1) * BLK, g * head_dim : (g + 1) * head_dim] for g in range(groups)],
                    axis=0,
                )
                m_blk = None
                for r, rels in enumerate(regions):
                    lo = local_index(rels[0])
                    k = k_ref[lo * BLK : (lo + len(rels)) * BLK, :]
                    sc = lax.dot_general(
                        k, q, (((1,), (1,)), ((), ())), preferred_element_type=jnp.float32
                    ) * score_scale
                    key = lax.broadcasted_iota(jnp.int32, sc.shape, 0) // BLK + rels[0]
                    keep = key >= start
                    if rels[-1] == i:
                        key_pos = lax.broadcasted_iota(jnp.int32, sc.shape, 0) + (rels[0] - i) * BLK
                        tok = lax.broadcasted_iota(jnp.int32, sc.shape, 1) % BLK
                        keep = keep & (key_pos <= tok)
                    sc = jnp.where(keep, sc, -jnp.inf)
                    s_sc[r, : len(rels) * BLK, :] = sc
                    mx = jnp.max(sc, axis=0, keepdims=True)
                    m_blk = mx if m_blk is None else jnp.maximum(m_blk, mx)
                if first:
                    m_new = m_blk
                    row_sum = jnp.zeros(m_new.shape, jnp.float32)
                    acc = jnp.zeros((head_dim, groups * BLK), jnp.float32)
                else:
                    m_old = m_in[i : i + 1, :]
                    m_new = jnp.maximum(m_old, m_blk)
                    alpha = jnp.exp(m_old - m_new)
                    row_sum = alpha * l_in[i : i + 1, :]
                    acc = alpha * acc_in[i]
                for r, rels in enumerate(regions):
                    p = jnp.exp(s_sc[r, : len(rels) * BLK, :] - m_new)
                    row_sum = row_sum + jnp.sum(p, axis=0, keepdims=True)
                    lo = local_index(rels[0])
                    v = v_ref[lo * BLK : (lo + len(rels)) * BLK, :]
                    acc = acc + lax.dot_general(
                        v, p.astype(jnp.bfloat16), (((0,), (0,)), ((), ())),
                        preferred_element_type=jnp.float32,
                    )
                finish(m_new, row_sum, acc)

            if first:
                compute()
            else:
                live = start <= regions[-1][-1]
                pl.when(live)(compute)
                pl.when(jnp.logical_not(live))(passthrough)

    return kernel


def doc_start_of(doc_blocks, blocks):
    ends = jnp.cumsum(doc_blocks)
    starts = ends - doc_blocks
    return jnp.max(jnp.where(starts[None, :] <= blocks[:, None], starts[None, :], 0), axis=1)


def on_device(queries, keys, values, doc_blocks):
    tok_rows, heads, qwidth = queries.shape
    head_dim = keys.shape[2]
    groups = qwidth // head_dim
    rows = groups * BLK
    dev_blocks = tok_rows // BLK
    score_scale = head_dim ** (-0.5)
    reach = min(4, lax.axis_size("seq") // 2)
    doc_blk = reach * dev_blocks
    firsts = [0] + [first_needed(r, reach, dev_blocks) for r in range(1, reach + 1)]

    device_pos = lax.axis_index("seq")
    first_block = device_pos * dev_blocks
    q_blocks = first_block + jnp.arange(dev_blocks, dtype=jnp.int32)
    rel_start = (doc_start_of(doc_blocks, q_blocks) - first_block).astype(jnp.int32)

    q2 = queries.reshape(tok_rows, heads * qwidth)
    k2 = keys.reshape(tok_rows, heads * head_dim)
    v2 = values.reshape(tok_rows, heads * head_dim)

    kv_cur = jnp.stack([k2, v2])
    kv_src = [kv_cur]
    prev_first = 0
    for r in range(1, reach + 1):
        cut = (firsts[r] - prev_first) * BLK
        kv_cur = shift_up(kv_cur[:, cut:], "seq")
        prev_first = firsts[r]
        kv_src.append(kv_cur)

    state_shapes = (
        jax.ShapeDtypeStruct((heads, dev_blocks, head_dim, rows), jnp.float32),
        jax.ShapeDtypeStruct((heads, dev_blocks, rows), jnp.float32),
        jax.ShapeDtypeStruct((heads, dev_blocks, rows), jnp.float32),
    )
    state_specs = [
        pl.BlockSpec((heads, dev_blocks, head_dim, rows), lambda h, rel: (0, 0, 0, 0)),
        pl.BlockSpec((heads, dev_blocks, rows), lambda h, rel: (0, 0, 0)),
        pl.BlockSpec((heads, dev_blocks, rows), lambda h, rel: (0, 0, 0)),
    ]
    scratch = [
        pltpu.VMEM((max(1, (dev_blocks + 1) // 2), 2 * BLK, rows), jnp.float32),
    ]
    q_spec = pl.BlockSpec((tok_rows, heads * qwidth), lambda h, rel: (0, 0))

    state = None
    out = None
    for stage in range(reach + 1):
        first = stage == 0
        last = stage == reach
        kernel = make_stage(stage, first, last, heads, dev_blocks, doc_blk, firsts, groups, head_dim, score_scale)
        kv_spec = pl.BlockSpec((2, kv_src[stage].shape[1], heads * head_dim), lambda h, rel: (0, 0, 0))
        in_specs = [q_spec, kv_spec] + ([] if first else state_specs)
        args = [rel_start, q2, kv_src[stage]] + ([] if first else list(state))
        if last:
            out_shape = jax.ShapeDtypeStruct((tok_rows, heads, qwidth), queries.dtype)
            out_specs = pl.BlockSpec((tok_rows, heads, qwidth), lambda h, rel: (0, 0, 0))
        else:
            out_shape = state_shapes
            out_specs = state_specs
        res = pl.pallas_call(
            kernel,
            out_shape=out_shape,
            grid_spec=pltpu.PrefetchScalarGridSpec(
                num_scalar_prefetch=1,
                grid=(1,),
                in_specs=in_specs,
                out_specs=out_specs,
                scratch_shapes=scratch + ([pltpu.VMEM((heads, dev_blocks, rows, head_dim), jnp.float32)] if last else []),
            ),
            compiler_params=pltpu.CompilerParams(dimension_semantics=("arbitrary",)),
        )(*args)
        if last:
            out = res
        else:
            state = res
    return out


def solution(mesh):
    placed = (
        P(("grp", "seq"), "head", None),
        P(("grp", "seq"), "head", None),
        P(("grp", "seq"), "head", None),
        P("grp"),
    )

    return jax.shard_map(
        on_device,
        mesh=mesh,
        in_specs=placed,
        out_specs=P(("grp", "seq"), "head", None),
        check_vma=False,
    )
```

```python
import jax
import jax.numpy as jnp
from jax import lax
from jax.experimental import pallas as pl
from jax.experimental.pallas import tpu as pltpu
from jax.sharding import PartitionSpec as P


BLK = 128


def shift_up(block, axis):
    size = lax.axis_size(axis)
    return lax.ppermute(block, axis, [(i, i + 1) for i in range(size - 1)])


def first_needed(distance, reach, dev_blocks):
    return max(0, (distance - reach) * dev_blocks + 1)


def stage_regions(stage, i, dev_blocks, doc_blk, firsts):
    if stage == 0:
        lo, hi = 0, i
    else:
        lo = -stage * dev_blocks + firsts[stage]
        hi = -(stage - 1) * dev_blocks - 1
    lo = max(lo, i - doc_blk + 1)
    rels = list(range(lo, hi + 1))
    regions = []
    while rels:
        take = 2 if len(rels) % 2 == 0 else 1
        regions.append(rels[:take])
        rels = rels[take:]
    return regions


def make_stage(stage, first, last, dev_blocks, doc_blk, firsts, groups, head_dim, score_scale):
    def local_index(rel):
        if stage == 0:
            return rel
        return rel + stage * dev_blocks - firsts[stage]

    def kernel(rel_ref, q_ref, kv_ref, *refs):
        k_ref = kv_ref.at[0]
        v_ref = kv_ref.at[1]
        if first:
            acc_in = m_in = l_in = None
            rest = refs
        else:
            acc_in, m_in, l_in = refs[:3]
            rest = refs[3:]
        if last:
            o_ref = rest[0]
            (s_sc,) = rest[1:]
        else:
            acc_out, m_out, l_out = rest[:3]
            (s_sc,) = rest[3:]

        for i in range(dev_blocks):
            start = rel_ref[i]
            regions = stage_regions(stage, i, dev_blocks, doc_blk, firsts)

            def finish(m_new, row_sum, acc):
                if last:
                    out = jnp.transpose(acc * (1.0 / row_sum))
                    for g in range(groups):
                        o_ref[i * BLK : (i + 1) * BLK, g * head_dim : (g + 1) * head_dim] = out[
                            g * BLK : (g + 1) * BLK
                        ].astype(o_ref.dtype)
                else:
                    acc_out[i] = acc
                    m_out[i : i + 1, :] = m_new
                    l_out[i : i + 1, :] = row_sum

            def passthrough():
                finish(m_in[i : i + 1, :], l_in[i : i + 1, :], acc_in[i])

            if not regions:
                passthrough()
                continue

            def compute():
                q = jnp.concatenate(
                    [q_ref[i * BLK : (i + 1) * BLK, g * head_dim : (g + 1) * head_dim] for g in range(groups)],
                    axis=0,
                )
                m_blk = None
                for r, rels in enumerate(regions):
                    lo = local_index(rels[0])
                    k = k_ref[lo * BLK : (lo + len(rels)) * BLK, :]
                    sc = lax.dot_general(
                        k, q, (((1,), (1,)), ((), ())), preferred_element_type=jnp.float32
                    ) * score_scale
                    key = lax.broadcasted_iota(jnp.int32, sc.shape, 0) // BLK + rels[0]
                    keep = key >= start
                    if rels[-1] == i:
                        key_pos = lax.broadcasted_iota(jnp.int32, sc.shape, 0) + (rels[0] - i) * BLK
                        tok = lax.broadcasted_iota(jnp.int32, sc.shape, 1) % BLK
                        keep = keep & (key_pos <= tok)
                    sc = jnp.where(keep, sc, -jnp.inf)
                    s_sc[r, : len(rels) * BLK, :] = sc
                    mx = jnp.max(sc, axis=0, keepdims=True)
                    m_blk = mx if m_blk is None else jnp.maximum(m_blk, mx)
                if first:
                    m_new = m_blk
                    row_sum = jnp.zeros(m_new.shape, jnp.float32)
                    acc = jnp.zeros((head_dim, groups * BLK), jnp.float32)
                else:
                    m_old = m_in[i : i + 1, :]
                    m_new = jnp.maximum(m_old, m_blk)
                    alpha = jnp.exp(m_old - m_new)
                    row_sum = alpha * l_in[i : i + 1, :]
                    acc = alpha * acc_in[i]
                for r, rels in enumerate(regions):
                    p = jnp.exp(s_sc[r, : len(rels) * BLK, :] - m_new)
                    row_sum = row_sum + jnp.sum(p, axis=0, keepdims=True)
                    lo = local_index(rels[0])
                    v = v_ref[lo * BLK : (lo + len(rels)) * BLK, :]
                    acc = acc + lax.dot_general(
                        v, p.astype(jnp.bfloat16), (((0,), (0,)), ((), ())),
                        preferred_element_type=jnp.float32,
                    )
                finish(m_new, row_sum, acc)

            if first:
                compute()
            else:
                live = start <= regions[-1][-1]
                pl.when(live)(compute)
                pl.when(jnp.logical_not(live))(passthrough)

    return kernel


def doc_start_of(doc_blocks, blocks):
    ends = jnp.cumsum(doc_blocks)
    starts = ends - doc_blocks
    return jnp.max(jnp.where(starts[None, :] <= blocks[:, None], starts[None, :], 0), axis=1)


def on_device(queries, keys, values, doc_blocks):
    tok_rows, heads, qwidth = queries.shape
    head_dim = keys.shape[2]
    groups = qwidth // head_dim
    rows = groups * BLK
    dev_blocks = tok_rows // BLK
    score_scale = head_dim ** (-0.5)
    reach = min(4, lax.axis_size("seq") // 2)
    doc_blk = reach * dev_blocks
    firsts = [0] + [first_needed(r, reach, dev_blocks) for r in range(1, reach + 1)]

    device_pos = lax.axis_index("seq")
    first_block = device_pos * dev_blocks
    q_blocks = first_block + jnp.arange(dev_blocks, dtype=jnp.int32)
    rel_start = (doc_start_of(doc_blocks, q_blocks) - first_block).astype(jnp.int32)

    q2 = queries.reshape(tok_rows, heads * qwidth)
    k2 = keys.reshape(tok_rows, heads * head_dim)
    v2 = values.reshape(tok_rows, heads * head_dim)

    kv_cur = jnp.stack([k2, v2])
    kv_src = [kv_cur]
    prev_first = 0
    split = firsts[2] * BLK if reach >= 2 else 0
    for r in range(1, reach + 1):
        cut = (firsts[r] - prev_first) * BLK
        if r == 1 and split > 0:
            tail = shift_up(kv_cur[:, split:], "seq")
            head = shift_up(kv_cur[:, :split], "seq")
            kv_src.append(jnp.concatenate([head, tail], axis=1))
            kv_cur = tail
            prev_first = firsts[2]
            continue
        kv_cur = shift_up(kv_cur[:, cut:], "seq")
        prev_first = firsts[r]
        kv_src.append(kv_cur)

    state_shapes = (
        jax.ShapeDtypeStruct((heads, dev_blocks, head_dim, rows), jnp.float32),
        jax.ShapeDtypeStruct((heads, dev_blocks, rows), jnp.float32),
        jax.ShapeDtypeStruct((heads, dev_blocks, rows), jnp.float32),
    )
    state_specs = [
        pl.BlockSpec((None, dev_blocks, head_dim, rows), lambda h, rel: (h, 0, 0, 0)),
        pl.BlockSpec((None, dev_blocks, rows), lambda h, rel: (h, 0, 0)),
        pl.BlockSpec((None, dev_blocks, rows), lambda h, rel: (h, 0, 0)),
    ]
    scratch = [
        pltpu.VMEM((max(1, (dev_blocks + 1) // 2), 2 * BLK, rows), jnp.float32),
    ]
    q_spec = pl.BlockSpec((tok_rows, qwidth), lambda h, rel: (0, h))

    state = None
    out = None
    for stage in range(reach + 1):
        first = stage == 0
        last = stage == reach
        kernel = make_stage(stage, first, last, dev_blocks, doc_blk, firsts, groups, head_dim, score_scale)
        kv_spec = pl.BlockSpec((2, kv_src[stage].shape[1], head_dim), lambda h, rel: (0, 0, h))
        in_specs = [q_spec, kv_spec] + ([] if first else state_specs)
        args = [rel_start, q2, kv_src[stage]] + ([] if first else list(state))
        if last:
            out_shape = jax.ShapeDtypeStruct((tok_rows, heads * qwidth), queries.dtype)
            out_specs = q_spec
        else:
            out_shape = state_shapes
            out_specs = state_specs
        res = pl.pallas_call(
            kernel,
            out_shape=out_shape,
            grid_spec=pltpu.PrefetchScalarGridSpec(
                num_scalar_prefetch=1,
                grid=(heads,),
                in_specs=in_specs,
                out_specs=out_specs,
                scratch_shapes=scratch,
            ),
            compiler_params=pltpu.CompilerParams(dimension_semantics=("arbitrary",)),
        )(*args)
        if last:
            out = res
        else:
            state = res
    return out.reshape(tok_rows, heads, qwidth)


def solution(mesh):
    placed = (
        P(("grp", "seq"), "head", None),
        P(("grp", "seq"), "head", None),
        P(("grp", "seq"), "head", None),
        P("grp"),
    )

    return jax.shard_map(
        on_device,
        mesh=mesh,
        in_specs=placed,
        out_specs=P(("grp", "seq"), "head", None),
        check_vma=False,
    )
```

```python
import jax
import jax.numpy as jnp
from jax import lax
from jax.experimental import pallas as pl
from jax.experimental.pallas import tpu as pltpu
from jax.sharding import PartitionSpec as P


BLK = 128


def shift_up(block, axis, distance=1):
    size = lax.axis_size(axis)
    return lax.ppermute(block, axis, [(i, i + distance) for i in range(size - distance)])


def first_needed(distance, reach, dev_blocks):
    return max(0, (distance - reach) * dev_blocks + 1)


def stage_regions(stage, i, dev_blocks, doc_blk, firsts):
    if stage == 0:
        lo, hi = 0, i
    else:
        lo = -stage * dev_blocks + firsts[stage]
        hi = -(stage - 1) * dev_blocks - 1
    lo = max(lo, i - doc_blk + 1)
    rels = list(range(lo, hi + 1))
    regions = []
    while rels:
        take = 2 if len(rels) % 2 == 0 else 1
        regions.append(rels[:take])
        rels = rels[take:]
    return regions


def make_stage(stage, first, last, dev_blocks, doc_blk, firsts, groups, head_dim, score_scale):
    def local_index(rel):
        if stage == 0:
            return rel
        return rel + stage * dev_blocks - firsts[stage]

    def kernel(rel_ref, q_ref, kv_ref, *refs):
        k_ref = kv_ref.at[0]
        v_ref = kv_ref.at[1]
        if first:
            acc_in = m_in = l_in = None
            rest = refs
        else:
            acc_in, m_in, l_in = refs[:3]
            rest = refs[3:]
        if last:
            o_ref = rest[0]
            (s_sc,) = rest[1:]
        else:
            acc_out, m_out, l_out = rest[:3]
            (s_sc,) = rest[3:]

        for i in range(dev_blocks):
            start = rel_ref[i]
            regions = stage_regions(stage, i, dev_blocks, doc_blk, firsts)

            def finish(m_new, row_sum, acc):
                if last:
                    out = jnp.transpose(acc * (1.0 / row_sum))
                    for g in range(groups):
                        o_ref[i * BLK : (i + 1) * BLK, g * head_dim : (g + 1) * head_dim] = out[
                            g * BLK : (g + 1) * BLK
                        ].astype(o_ref.dtype)
                else:
                    acc_out[i] = acc
                    m_out[i : i + 1, :] = m_new
                    l_out[i : i + 1, :] = row_sum

            def passthrough():
                finish(m_in[i : i + 1, :], l_in[i : i + 1, :], acc_in[i])

            if not regions:
                passthrough()
                continue

            def compute():
                q = jnp.concatenate(
                    [q_ref[i * BLK : (i + 1) * BLK, g * head_dim : (g + 1) * head_dim] for g in range(groups)],
                    axis=0,
                )
                m_blk = None
                for r, rels in enumerate(regions):
                    lo = local_index(rels[0])
                    k = k_ref[lo * BLK : (lo + len(rels)) * BLK, :]
                    sc = lax.dot_general(
                        k, q, (((1,), (1,)), ((), ())), preferred_element_type=jnp.float32
                    ) * score_scale
                    key = lax.broadcasted_iota(jnp.int32, sc.shape, 0) // BLK + rels[0]
                    keep = key >= start
                    if rels[-1] == i:
                        key_pos = lax.broadcasted_iota(jnp.int32, sc.shape, 0) + (rels[0] - i) * BLK
                        tok = lax.broadcasted_iota(jnp.int32, sc.shape, 1) % BLK
                        keep = keep & (key_pos <= tok)
                    sc = jnp.where(keep, sc, -jnp.inf)
                    s_sc[r, : len(rels) * BLK, :] = sc
                    mx = jnp.max(sc, axis=0, keepdims=True)
                    m_blk = mx if m_blk is None else jnp.maximum(m_blk, mx)
                if first:
                    m_new = m_blk
                    row_sum = jnp.zeros(m_new.shape, jnp.float32)
                    acc = jnp.zeros((head_dim, groups * BLK), jnp.float32)
                else:
                    m_old = m_in[i : i + 1, :]
                    m_new = jnp.maximum(m_old, m_blk)
                    alpha = jnp.exp(m_old - m_new)
                    row_sum = alpha * l_in[i : i + 1, :]
                    acc = alpha * acc_in[i]
                for r, rels in enumerate(regions):
                    p = jnp.exp(s_sc[r, : len(rels) * BLK, :] - m_new)
                    row_sum = row_sum + jnp.sum(p, axis=0, keepdims=True)
                    lo = local_index(rels[0])
                    v = v_ref[lo * BLK : (lo + len(rels)) * BLK, :]
                    acc = acc + lax.dot_general(
                        v, p.astype(jnp.bfloat16), (((0,), (0,)), ((), ())),
                        preferred_element_type=jnp.float32,
                    )
                finish(m_new, row_sum, acc)

            if first:
                compute()
            else:
                live = start <= regions[-1][-1]
                pl.when(live)(compute)
                pl.when(jnp.logical_not(live))(passthrough)

    return kernel


def doc_start_of(doc_blocks, blocks):
    ends = jnp.cumsum(doc_blocks)
    starts = ends - doc_blocks
    return jnp.max(jnp.where(starts[None, :] <= blocks[:, None], starts[None, :], 0), axis=1)


def on_device(queries, keys, values, doc_blocks):
    tok_rows, heads, qwidth = queries.shape
    head_dim = keys.shape[2]
    groups = qwidth // head_dim
    rows = groups * BLK
    dev_blocks = tok_rows // BLK
    score_scale = head_dim ** (-0.5)
    reach = min(4, lax.axis_size("seq") // 2)
    doc_blk = reach * dev_blocks
    firsts = [0] + [first_needed(r, reach, dev_blocks) for r in range(1, reach + 1)]

    device_pos = lax.axis_index("seq")
    first_block = device_pos * dev_blocks
    q_blocks = first_block + jnp.arange(dev_blocks, dtype=jnp.int32)
    rel_start = (doc_start_of(doc_blocks, q_blocks) - first_block).astype(jnp.int32)

    q2 = queries.reshape(tok_rows, heads * qwidth)
    k2 = keys.reshape(tok_rows, heads * head_dim)
    v2 = values.reshape(tok_rows, heads * head_dim)

    kv_own = jnp.stack([k2, v2])
    kv_src = [kv_own]
    for r in range(1, reach + 1):
        kv_src.append(shift_up(kv_own[:, firsts[r] * BLK :], "seq", r))

    state_shapes = (
        jax.ShapeDtypeStruct((heads, dev_blocks, head_dim, rows), jnp.float32),
        jax.ShapeDtypeStruct((heads, dev_blocks, rows), jnp.float32),
        jax.ShapeDtypeStruct((heads, dev_blocks, rows), jnp.float32),
    )
    state_specs = [
        pl.BlockSpec((None, dev_blocks, head_dim, rows), lambda h, rel: (h, 0, 0, 0)),
        pl.BlockSpec((None, dev_blocks, rows), lambda h, rel: (h, 0, 0)),
        pl.BlockSpec((None, dev_blocks, rows), lambda h, rel: (h, 0, 0)),
    ]
    scratch = [
        pltpu.VMEM((max(1, (dev_blocks + 1) // 2), 2 * BLK, rows), jnp.float32),
    ]
    q_spec = pl.BlockSpec((tok_rows, qwidth), lambda h, rel: (0, h))

    state = None
    out = None
    for stage in range(reach + 1):
        first = stage == 0
        last = stage == reach
        kernel = make_stage(stage, first, last, dev_blocks, doc_blk, firsts, groups, head_dim, score_scale)
        kv_spec = pl.BlockSpec((2, kv_src[stage].shape[1], head_dim), lambda h, rel: (0, 0, h))
        in_specs = [q_spec, kv_spec] + ([] if first else state_specs)
        args = [rel_start, q2, kv_src[stage]] + ([] if first else list(state))
        if last:
            out_shape = jax.ShapeDtypeStruct((tok_rows, heads * qwidth), queries.dtype)
            out_specs = q_spec
        else:
            out_shape = state_shapes
            out_specs = state_specs
        res = pl.pallas_call(
            kernel,
            out_shape=out_shape,
            grid_spec=pltpu.PrefetchScalarGridSpec(
                num_scalar_prefetch=1,
                grid=(heads,),
                in_specs=in_specs,
                out_specs=out_specs,
                scratch_shapes=scratch,
            ),
            compiler_params=pltpu.CompilerParams(dimension_semantics=("arbitrary",)),
        )(*args)
        if last:
            out = res
        else:
            state = res
    return out.reshape(tok_rows, heads, qwidth)


def solution(mesh):
    placed = (
        P(("grp", "seq"), "head", None),
        P(("grp", "seq"), "head", None),
        P(("grp", "seq"), "head", None),
        P("grp"),
    )

    return jax.shard_map(
        on_device,
        mesh=mesh,
        in_specs=placed,
        out_specs=P(("grp", "seq"), "head", None),
        check_vma=False,
    )
```

```python
import jax
import jax.numpy as jnp
from jax import lax
from jax.experimental import pallas as pl
from jax.experimental.pallas import tpu as pltpu
from jax.sharding import PartitionSpec as P


BLK = 128


def shift_up(block, axis):
    size = lax.axis_size(axis)
    return lax.ppermute(block, axis, [(i, i + 1) for i in range(size - 1)])


def first_needed(distance, reach, dev_blocks):
    return max(0, (distance - reach) * dev_blocks + 1)


def stage_regions(stage, i, dev_blocks, doc_blk, firsts):
    if stage == 0:
        lo, hi = 0, i
    else:
        lo = -stage * dev_blocks + firsts[stage]
        hi = -(stage - 1) * dev_blocks - 1
    lo = max(lo, i - doc_blk + 1)
    rels = list(range(lo, hi + 1))
    regions = []
    while rels:
        take = 2 if len(rels) % 2 == 0 else 1
        regions.append(rels[:take])
        rels = rels[take:]
    return regions


def make_stage(stage, first, last, provisional, dev_blocks, doc_blk, firsts, groups, head_dim, score_scale):
    def local_index(rel):
        if stage == 0:
            return rel
        return rel + stage * dev_blocks - firsts[stage]

    def kernel(rel_ref, q_ref, kv_ref, *refs):
        k_ref = kv_ref.at[0]
        v_ref = kv_ref.at[1]
        if first:
            acc_in = m_in = l_in = None
            rest = refs
        else:
            acc_in, m_in, l_in = refs[:3]
            rest = refs[3:]
        if last:
            o_ref = rest[0]
            (s_sc,) = rest[1:]
        elif provisional:
            acc_out, m_out, l_out, o_ref = rest[:4]
            (s_sc,) = rest[4:]
        else:
            acc_out, m_out, l_out = rest[:3]
            (s_sc,) = rest[3:]

        for i in range(dev_blocks):
            start = rel_ref[i]
            regions = stage_regions(stage, i, dev_blocks, doc_blk, firsts)

            def finish(m_new, row_sum, acc):
                if last or provisional:
                    out = jnp.transpose(acc * (1.0 / row_sum))
                    for g in range(groups):
                        o_ref[i * BLK : (i + 1) * BLK, g * head_dim : (g + 1) * head_dim] = out[
                            g * BLK : (g + 1) * BLK
                        ].astype(o_ref.dtype)
                if not last:
                    acc_out[i] = acc
                    m_out[i : i + 1, :] = m_new
                    l_out[i : i + 1, :] = row_sum

            def passthrough():
                finish(m_in[i : i + 1, :], l_in[i : i + 1, :], acc_in[i])

            if not regions:
                passthrough()
                continue

            def compute():
                q = jnp.concatenate(
                    [q_ref[i * BLK : (i + 1) * BLK, g * head_dim : (g + 1) * head_dim] for g in range(groups)],
                    axis=0,
                )
                m_blk = None
                for r, rels in enumerate(regions):
                    lo = local_index(rels[0])
                    k = k_ref[lo * BLK : (lo + len(rels)) * BLK, :]
                    sc = lax.dot_general(
                        k, q, (((1,), (1,)), ((), ())), preferred_element_type=jnp.float32
                    ) * score_scale
                    key = lax.broadcasted_iota(jnp.int32, sc.shape, 0) // BLK + rels[0]
                    keep = key >= start
                    if rels[-1] == i:
                        key_pos = lax.broadcasted_iota(jnp.int32, sc.shape, 0) + (rels[0] - i) * BLK
                        tok = lax.broadcasted_iota(jnp.int32, sc.shape, 1) % BLK
                        keep = keep & (key_pos <= tok)
                    sc = jnp.where(keep, sc, -jnp.inf)
                    s_sc[r, : len(rels) * BLK, :] = sc
                    mx = jnp.max(sc, axis=0, keepdims=True)
                    m_blk = mx if m_blk is None else jnp.maximum(m_blk, mx)
                if first:
                    m_new = m_blk
                    row_sum = jnp.zeros(m_new.shape, jnp.float32)
                    acc = jnp.zeros((head_dim, groups * BLK), jnp.float32)
                else:
                    m_old = m_in[i : i + 1, :]
                    m_new = jnp.maximum(m_old, m_blk)
                    alpha = jnp.exp(m_old - m_new)
                    row_sum = alpha * l_in[i : i + 1, :]
                    acc = alpha * acc_in[i]
                for r, rels in enumerate(regions):
                    p = jnp.exp(s_sc[r, : len(rels) * BLK, :] - m_new)
                    row_sum = row_sum + jnp.sum(p, axis=0, keepdims=True)
                    lo = local_index(rels[0])
                    v = v_ref[lo * BLK : (lo + len(rels)) * BLK, :]
                    acc = acc + lax.dot_general(
                        v, p.astype(jnp.bfloat16), (((0,), (0,)), ((), ())),
                        preferred_element_type=jnp.float32,
                    )
                finish(m_new, row_sum, acc)

            if first:
                compute()
            else:
                live = start <= regions[-1][-1]
                pl.when(live)(compute)
                pl.when(jnp.logical_not(live))(passthrough)

    return kernel


def make_patch(stage, heads, dev_blocks, doc_blk, firsts, groups, head_dim, score_scale):
    qwidth = groups * head_dim

    def local_index(rel):
        return rel + stage * dev_blocks - firsts[stage]

    def kernel(rel_ref, q_hbm, kv_ref, acc_hbm, m_hbm, l_hbm, prov_hbm, out_hbm,
               q_buf, acc_buf, m_buf, l_buf, s_sc, o_f32, o_buf, sems):
        del prov_hbm
        for i in range(dev_blocks):
            regions = stage_regions(stage, i, dev_blocks, doc_blk, firsts)
            if not regions:
                continue
            start = rel_ref[i]

            def patch_block():
                copies = [
                    pltpu.make_async_copy(q_hbm.at[pl.ds(i * BLK, BLK)], q_buf, sems.at[0]),
                    pltpu.make_async_copy(acc_hbm.at[:, i], acc_buf, sems.at[1]),
                    pltpu.make_async_copy(m_hbm.at[:, pl.ds(i, 1)], m_buf, sems.at[2]),
                    pltpu.make_async_copy(l_hbm.at[:, pl.ds(i, 1)], l_buf, sems.at[3]),
                ]
                for c in copies:
                    c.start()
                for c in copies:
                    c.wait()
                for h in range(heads):
                    q = jnp.concatenate(
                        [q_buf[:, h * qwidth + g * head_dim : h * qwidth + (g + 1) * head_dim] for g in range(groups)],
                        axis=0,
                    )
                    m_blk = None
                    for r, rels in enumerate(regions):
                        lo = local_index(rels[0])
                        k = kv_ref[0, lo * BLK : (lo + len(rels)) * BLK, h * head_dim : (h + 1) * head_dim]
                        sc = lax.dot_general(
                            k, q, (((1,), (1,)), ((), ())), preferred_element_type=jnp.float32
                        ) * score_scale
                        key = lax.broadcasted_iota(jnp.int32, sc.shape, 0) // BLK + rels[0]
                        sc = jnp.where(key >= start, sc, -jnp.inf)
                        s_sc[r, : len(rels) * BLK, :] = sc
                        mx = jnp.max(sc, axis=0, keepdims=True)
                        m_blk = mx if m_blk is None else jnp.maximum(m_blk, mx)
                    m_old = m_buf[h]
                    m_new = jnp.maximum(m_old, m_blk)
                    alpha = jnp.exp(m_old - m_new)
                    row_sum = alpha * l_buf[h]
                    acc = alpha * acc_buf[h]
                    for r, rels in enumerate(regions):
                        p = jnp.exp(s_sc[r, : len(rels) * BLK, :] - m_new)
                        row_sum = row_sum + jnp.sum(p, axis=0, keepdims=True)
                        lo = local_index(rels[0])
                        v = kv_ref[1, lo * BLK : (lo + len(rels)) * BLK, h * head_dim : (h + 1) * head_dim]
                        acc = acc + lax.dot_general(
                            v, p.astype(jnp.bfloat16), (((0,), (0,)), ((), ())),
                            preferred_element_type=jnp.float32,
                        )
                    o_f32[h] = jnp.transpose(acc * (1.0 / row_sum))
                for g in range(groups):
                    vals = jnp.stack([o_f32[h, g * BLK : (g + 1) * BLK, :] for h in range(heads)], axis=1)
                    o_buf[:, :, g * head_dim : (g + 1) * head_dim] = vals.astype(o_buf.dtype)
                out_copy = pltpu.make_async_copy(o_buf, out_hbm.at[pl.ds(i * BLK, BLK)], sems.at[4])
                out_copy.start()
                out_copy.wait()

            pl.when(start <= regions[-1][-1])(patch_block)

    return kernel


def doc_start_of(doc_blocks, blocks):
    ends = jnp.cumsum(doc_blocks)
    starts = ends - doc_blocks
    return jnp.max(jnp.where(starts[None, :] <= blocks[:, None], starts[None, :], 0), axis=1)


def on_device(queries, keys, values, doc_blocks):
    tok_rows, heads, qwidth = queries.shape
    head_dim = keys.shape[2]
    groups = qwidth // head_dim
    rows = groups * BLK
    dev_blocks = tok_rows // BLK
    score_scale = head_dim ** (-0.5)
    reach = min(4, lax.axis_size("seq") // 2)
    doc_blk = reach * dev_blocks
    firsts = [0] + [first_needed(r, reach, dev_blocks) for r in range(1, reach + 1)]

    device_pos = lax.axis_index("seq")
    first_block = device_pos * dev_blocks
    q_blocks = first_block + jnp.arange(dev_blocks, dtype=jnp.int32)
    rel_start = (doc_start_of(doc_blocks, q_blocks) - first_block).astype(jnp.int32)

    q2 = queries.reshape(tok_rows, heads * qwidth)
    k2 = keys.reshape(tok_rows, heads * head_dim)
    v2 = values.reshape(tok_rows, heads * head_dim)

    kv_cur = jnp.stack([k2, v2])
    kv_src = [kv_cur]
    prev_first = 0
    for r in range(1, reach + 1):
        cut = (firsts[r] - prev_first) * BLK
        kv_cur = shift_up(kv_cur[:, cut:], "seq")
        prev_first = firsts[r]
        kv_src.append(kv_cur)

    state_shapes = (
        jax.ShapeDtypeStruct((heads, dev_blocks, head_dim, rows), jnp.float32),
        jax.ShapeDtypeStruct((heads, dev_blocks, rows), jnp.float32),
        jax.ShapeDtypeStruct((heads, dev_blocks, rows), jnp.float32),
    )
    state_specs = [
        pl.BlockSpec((None, dev_blocks, head_dim, rows), lambda h, rel: (h, 0, 0, 0)),
        pl.BlockSpec((None, dev_blocks, rows), lambda h, rel: (h, 0, 0)),
        pl.BlockSpec((None, dev_blocks, rows), lambda h, rel: (h, 0, 0)),
    ]
    scratch = [
        pltpu.VMEM((max(1, (dev_blocks + 1) // 2), 2 * BLK, rows), jnp.float32),
    ]
    q_spec = pl.BlockSpec((tok_rows, qwidth), lambda h, rel: (0, h))

    state = None
    out = None
    for stage in range(reach):
        first = stage == 0
        last = False
        provisional = stage == reach - 1
        kernel = make_stage(stage, first, last, provisional, dev_blocks, doc_blk, firsts, groups, head_dim, score_scale)
        kv_spec = pl.BlockSpec((2, kv_src[stage].shape[1], head_dim), lambda h, rel: (0, 0, h))
        in_specs = [q_spec, kv_spec] + ([] if first else state_specs)
        args = [rel_start, q2, kv_src[stage]] + ([] if first else list(state))
        out_shape = state_shapes
        out_specs = state_specs
        if provisional:
            out_shape = state_shapes + (jax.ShapeDtypeStruct((tok_rows, heads * qwidth), queries.dtype),)
            out_specs = state_specs + [q_spec]
        res = pl.pallas_call(
            kernel,
            out_shape=out_shape,
            grid_spec=pltpu.PrefetchScalarGridSpec(
                num_scalar_prefetch=1,
                grid=(heads,),
                in_specs=in_specs,
                out_specs=out_specs,
                scratch_shapes=scratch,
            ),
            compiler_params=pltpu.CompilerParams(dimension_semantics=("arbitrary",)),
        )(*args)
        state = res[:3]
        if provisional:
            out = res[3].reshape(tok_rows, heads, qwidth)

    n_regions = max(1, (dev_blocks + 1) // 2)
    any_spec = pl.BlockSpec(memory_space=pl.ANY)
    kv_last = kv_src[reach]
    out = pl.pallas_call(
        make_patch(reach, heads, dev_blocks, doc_blk, firsts, groups, head_dim, score_scale),
        out_shape=jax.ShapeDtypeStruct((tok_rows, heads, qwidth), queries.dtype),
        grid_spec=pltpu.PrefetchScalarGridSpec(
            num_scalar_prefetch=1,
            grid=(1,),
            in_specs=[
                any_spec,
                pl.BlockSpec(kv_last.shape, lambda h, rel: (0, 0, 0)),
                any_spec,
                any_spec,
                any_spec,
                any_spec,
            ],
            out_specs=any_spec,
            scratch_shapes=[
                pltpu.VMEM((BLK, heads * qwidth), queries.dtype),
                pltpu.VMEM((heads, head_dim, rows), jnp.float32),
                pltpu.VMEM((heads, 1, rows), jnp.float32),
                pltpu.VMEM((heads, 1, rows), jnp.float32),
                pltpu.VMEM((n_regions, 2 * BLK, rows), jnp.float32),
                pltpu.VMEM((heads, rows, head_dim), jnp.float32),
                pltpu.VMEM((BLK, heads, qwidth), queries.dtype),
                pltpu.SemaphoreType.DMA((5,)),
            ],
        ),
        input_output_aliases={6: 0},
    )(rel_start, q2, kv_last, *state, out)
    return out


def solution(mesh):
    placed = (
        P(("grp", "seq"), "head", None),
        P(("grp", "seq"), "head", None),
        P(("grp", "seq"), "head", None),
        P("grp"),
    )

    return jax.shard_map(
        on_device,
        mesh=mesh,
        in_specs=placed,
        out_specs=P(("grp", "seq"), "head", None),
        check_vma=False,
    )
```

```python
import jax
import jax.numpy as jnp
from jax import lax
from jax.experimental import pallas as pl
from jax.experimental.pallas import tpu as pltpu
from jax.sharding import PartitionSpec as P


BLK = 128


def shift_up(block, axis):
    size = lax.axis_size(axis)
    return lax.ppermute(block, axis, [(i, i + 1) for i in range(size - 1)])


def first_needed(distance, reach, dev_blocks):
    return max(0, (distance - reach) * dev_blocks + 1)


def stage_regions(stage, i, dev_blocks, doc_blk, firsts):
    if stage == 0:
        lo, hi = 0, i
    else:
        lo = -stage * dev_blocks + firsts[stage]
        hi = -(stage - 1) * dev_blocks - 1
    lo = max(lo, i - doc_blk + 1)
    rels = list(range(lo, hi + 1))
    regions = []
    while rels:
        take = 2 if len(rels) % 2 == 0 else 1
        regions.append(rels[:take])
        rels = rels[take:]
    return regions


def make_stage(stage, first, last, provisional, dev_blocks, doc_blk, firsts, groups, head_dim, score_scale):
    def local_index(rel):
        if stage == 0:
            return rel
        return rel + stage * dev_blocks - firsts[stage]

    def kernel(rel_ref, q_ref, kv_ref, *refs):
        k_ref = kv_ref.at[0]
        v_ref = kv_ref.at[1]
        if first:
            acc_in = m_in = l_in = None
            rest = refs
        else:
            acc_in, m_in, l_in = refs[:3]
            rest = refs[3:]
        if last:
            o_ref = rest[0]
            (s_sc,) = rest[1:]
        elif provisional:
            acc_out, m_out, l_out, o_ref = rest[:4]
            (s_sc,) = rest[4:]
        else:
            acc_out, m_out, l_out = rest[:3]
            (s_sc,) = rest[3:]

        for i in range(dev_blocks):
            start = rel_ref[i]
            regions = stage_regions(stage, i, dev_blocks, doc_blk, firsts)

            def finish(m_new, row_sum, acc):
                if last or provisional:
                    out = jnp.transpose(acc * (1.0 / row_sum))
                    for g in range(groups):
                        o_ref[i * BLK : (i + 1) * BLK, g * head_dim : (g + 1) * head_dim] = out[
                            g * BLK : (g + 1) * BLK
                        ].astype(o_ref.dtype)
                if not last:
                    acc_out[i] = acc
                    m_out[i : i + 1, :] = m_new
                    l_out[i : i + 1, :] = row_sum

            def passthrough():
                finish(m_in[i : i + 1, :], l_in[i : i + 1, :], acc_in[i])

            if not regions:
                passthrough()
                continue

            def compute():
                q = jnp.concatenate(
                    [q_ref[i * BLK : (i + 1) * BLK, g * head_dim : (g + 1) * head_dim] for g in range(groups)],
                    axis=0,
                )
                m_blk = None
                for r, rels in enumerate(regions):
                    lo = local_index(rels[0])
                    k = k_ref[lo * BLK : (lo + len(rels)) * BLK, :]
                    sc = lax.dot_general(
                        k, q, (((1,), (1,)), ((), ())), preferred_element_type=jnp.float32
                    ) * score_scale
                    key = lax.broadcasted_iota(jnp.int32, sc.shape, 0) // BLK + rels[0]
                    keep = key >= start
                    if rels[-1] == i:
                        key_pos = lax.broadcasted_iota(jnp.int32, sc.shape, 0) + (rels[0] - i) * BLK
                        tok = lax.broadcasted_iota(jnp.int32, sc.shape, 1) % BLK
                        keep = keep & (key_pos <= tok)
                    sc = jnp.where(keep, sc, -jnp.inf)
                    s_sc[r, : len(rels) * BLK, :] = sc
                    mx = jnp.max(sc, axis=0, keepdims=True)
                    m_blk = mx if m_blk is None else jnp.maximum(m_blk, mx)
                if first:
                    m_new = m_blk
                    row_sum = jnp.zeros(m_new.shape, jnp.float32)
                    acc = jnp.zeros((head_dim, groups * BLK), jnp.float32)
                else:
                    m_old = m_in[i : i + 1, :]
                    m_new = jnp.maximum(m_old, m_blk)
                    alpha = jnp.exp(m_old - m_new)
                    row_sum = alpha * l_in[i : i + 1, :]
                    acc = alpha * acc_in[i]
                for r, rels in enumerate(regions):
                    p = jnp.exp(s_sc[r, : len(rels) * BLK, :] - m_new)
                    row_sum = row_sum + jnp.sum(p, axis=0, keepdims=True)
                    lo = local_index(rels[0])
                    v = v_ref[lo * BLK : (lo + len(rels)) * BLK, :]
                    acc = acc + lax.dot_general(
                        v, p.astype(jnp.bfloat16), (((0,), (0,)), ((), ())),
                        preferred_element_type=jnp.float32,
                    )
                finish(m_new, row_sum, acc)

            if first:
                compute()
            else:
                live = start <= regions[-1][-1]
                pl.when(live)(compute)
                pl.when(jnp.logical_not(live))(passthrough)

    return kernel


def make_patch(stage, heads, dev_blocks, doc_blk, firsts, groups, head_dim, score_scale):
    qwidth = groups * head_dim

    def local_index(rel):
        return rel + stage * dev_blocks - firsts[stage]

    def kernel(rel_ref, q_hbm, kv_hbm, acc_hbm, m_hbm, l_hbm, prov_hbm, out_hbm,
               kv_buf, q_buf, acc_buf, m_buf, l_buf, s_sc, o_f32, o_buf, kv_sem, sems):
        del prov_hbm
        blocks = []
        for i in range(dev_blocks):
            regions = stage_regions(stage, i, dev_blocks, doc_blk, firsts)
            if regions:
                blocks.append((i, regions, rel_ref[i] <= regions[-1][-1]))
        if not blocks:
            return
        any_live = blocks[0][2]
        for _, _, live in blocks[1:]:
            any_live = jnp.logical_or(any_live, live)
        kv_copy = pltpu.make_async_copy(kv_hbm, kv_buf, kv_sem.at[0])

        def block_copies(i):
            return [
                pltpu.make_async_copy(q_hbm.at[pl.ds(i * BLK, BLK)], q_buf.at[i], sems.at[i, 0]),
                pltpu.make_async_copy(acc_hbm.at[:, i], acc_buf.at[i], sems.at[i, 1]),
                pltpu.make_async_copy(m_hbm.at[:, pl.ds(i, 1)], m_buf.at[i], sems.at[i, 2]),
                pltpu.make_async_copy(l_hbm.at[:, pl.ds(i, 1)], l_buf.at[i], sems.at[i, 3]),
            ]

        def out_copy(i):
            return pltpu.make_async_copy(o_buf.at[i], out_hbm.at[pl.ds(i * BLK, BLK)], sems.at[i, 4])

        pl.when(any_live)(kv_copy.start)
        for i, _, live in blocks:
            @pl.when(live)
            def _():
                for c in block_copies(i):
                    c.start()
        pl.when(any_live)(kv_copy.wait)

        for i, regions, live in blocks:
            start = rel_ref[i]

            def patch_block():
                for c in block_copies(i):
                    c.wait()
                for h in range(heads):
                    q = jnp.concatenate(
                        [q_buf[i, :, h * qwidth + g * head_dim : h * qwidth + (g + 1) * head_dim] for g in range(groups)],
                        axis=0,
                    )
                    m_blk = None
                    for r, rels in enumerate(regions):
                        lo = local_index(rels[0])
                        k = kv_buf[0, lo * BLK : (lo + len(rels)) * BLK, h * head_dim : (h + 1) * head_dim]
                        sc = lax.dot_general(
                            k, q, (((1,), (1,)), ((), ())), preferred_element_type=jnp.float32
                        ) * score_scale
                        key = lax.broadcasted_iota(jnp.int32, sc.shape, 0) // BLK + rels[0]
                        sc = jnp.where(key >= start, sc, -jnp.inf)
                        s_sc[r, : len(rels) * BLK, :] = sc
                        mx = jnp.max(sc, axis=0, keepdims=True)
                        m_blk = mx if m_blk is None else jnp.maximum(m_blk, mx)
                    m_old = m_buf[i, h]
                    m_new = jnp.maximum(m_old, m_blk)
                    alpha = jnp.exp(m_old - m_new)
                    row_sum = alpha * l_buf[i, h]
                    acc = alpha * acc_buf[i, h]
                    for r, rels in enumerate(regions):
                        p = jnp.exp(s_sc[r, : len(rels) * BLK, :] - m_new)
                        row_sum = row_sum + jnp.sum(p, axis=0, keepdims=True)
                        lo = local_index(rels[0])
                        v = kv_buf[1, lo * BLK : (lo + len(rels)) * BLK, h * head_dim : (h + 1) * head_dim]
                        acc = acc + lax.dot_general(
                            v, p.astype(jnp.bfloat16), (((0,), (0,)), ((), ())),
                            preferred_element_type=jnp.float32,
                        )
                    o_f32[h] = jnp.transpose(acc * (1.0 / row_sum))
                for g in range(groups):
                    vals = jnp.stack([o_f32[h, g * BLK : (g + 1) * BLK, :] for h in range(heads)], axis=1)
                    o_buf[i, :, :, g * head_dim : (g + 1) * head_dim] = vals.astype(o_buf.dtype)
                out_copy(i).start()

            pl.when(live)(patch_block)

        for i, _, live in blocks:
            pl.when(live)(out_copy(i).wait)

    return kernel


def doc_start_of(doc_blocks, blocks):
    ends = jnp.cumsum(doc_blocks)
    starts = ends - doc_blocks
    return jnp.max(jnp.where(starts[None, :] <= blocks[:, None], starts[None, :], 0), axis=1)


def on_device(queries, keys, values, doc_blocks):
    tok_rows, heads, qwidth = queries.shape
    head_dim = keys.shape[2]
    groups = qwidth // head_dim
    rows = groups * BLK
    dev_blocks = tok_rows // BLK
    score_scale = head_dim ** (-0.5)
    reach = min(4, lax.axis_size("seq") // 2)
    doc_blk = reach * dev_blocks
    firsts = [0] + [first_needed(r, reach, dev_blocks) for r in range(1, reach + 1)]

    device_pos = lax.axis_index("seq")
    first_block = device_pos * dev_blocks
    q_blocks = first_block + jnp.arange(dev_blocks, dtype=jnp.int32)
    rel_start = (doc_start_of(doc_blocks, q_blocks) - first_block).astype(jnp.int32)

    q2 = queries.reshape(tok_rows, heads * qwidth)
    k2 = keys.reshape(tok_rows, heads * head_dim)
    v2 = values.reshape(tok_rows, heads * head_dim)

    kv_cur = jnp.stack([k2, v2])
    kv_src = [kv_cur]
    prev_first = 0
    for r in range(1, reach + 1):
        cut = (firsts[r] - prev_first) * BLK
        kv_cur = shift_up(kv_cur[:, cut:], "seq")
        prev_first = firsts[r]
        kv_src.append(kv_cur)

    state_shapes = (
        jax.ShapeDtypeStruct((heads, dev_blocks, head_dim, rows), jnp.float32),
        jax.ShapeDtypeStruct((heads, dev_blocks, rows), jnp.float32),
        jax.ShapeDtypeStruct((heads, dev_blocks, rows), jnp.float32),
    )
    state_specs = [
        pl.BlockSpec((None, dev_blocks, head_dim, rows), lambda h, rel: (h, 0, 0, 0)),
        pl.BlockSpec((None, dev_blocks, rows), lambda h, rel: (h, 0, 0)),
        pl.BlockSpec((None, dev_blocks, rows), lambda h, rel: (h, 0, 0)),
    ]
    scratch = [
        pltpu.VMEM((max(1, (dev_blocks + 1) // 2), 2 * BLK, rows), jnp.float32),
    ]
    q_spec = pl.BlockSpec((tok_rows, qwidth), lambda h, rel: (0, h))

    state = None
    out = None
    for stage in range(reach):
        first = stage == 0
        last = False
        provisional = stage == reach - 1
        kernel = make_stage(stage, first, last, provisional, dev_blocks, doc_blk, firsts, groups, head_dim, score_scale)
        kv_spec = pl.BlockSpec((2, kv_src[stage].shape[1], head_dim), lambda h, rel: (0, 0, h))
        in_specs = [q_spec, kv_spec] + ([] if first else state_specs)
        args = [rel_start, q2, kv_src[stage]] + ([] if first else list(state))
        out_shape = state_shapes
        out_specs = state_specs
        if provisional:
            out_shape = state_shapes + (jax.ShapeDtypeStruct((tok_rows, heads * qwidth), queries.dtype),)
            out_specs = state_specs + [q_spec]
        res = pl.pallas_call(
            kernel,
            out_shape=out_shape,
            grid_spec=pltpu.PrefetchScalarGridSpec(
                num_scalar_prefetch=1,
                grid=(heads,),
                in_specs=in_specs,
                out_specs=out_specs,
                scratch_shapes=scratch,
            ),
            compiler_params=pltpu.CompilerParams(dimension_semantics=("arbitrary",)),
        )(*args)
        state = res[:3]
        if provisional:
            out = res[3].reshape(tok_rows, heads, qwidth)

    n_regions = max(1, (dev_blocks + 1) // 2)
    any_spec = pl.BlockSpec(memory_space=pl.ANY)
    kv_last = kv_src[reach]
    out = pl.pallas_call(
        make_patch(reach, heads, dev_blocks, doc_blk, firsts, groups, head_dim, score_scale),
        out_shape=jax.ShapeDtypeStruct((tok_rows, heads, qwidth), queries.dtype),
        grid_spec=pltpu.PrefetchScalarGridSpec(
            num_scalar_prefetch=1,
            grid=(1,),
            in_specs=[
                any_spec,
                any_spec,
                any_spec,
                any_spec,
                any_spec,
                any_spec,
            ],
            out_specs=any_spec,
            scratch_shapes=[
                pltpu.VMEM(kv_last.shape, kv_last.dtype),
                pltpu.VMEM((dev_blocks, BLK, heads * qwidth), queries.dtype),
                pltpu.VMEM((dev_blocks, heads, head_dim, rows), jnp.float32),
                pltpu.VMEM((dev_blocks, heads, 1, rows), jnp.float32),
                pltpu.VMEM((dev_blocks, heads, 1, rows), jnp.float32),
                pltpu.VMEM((n_regions, 2 * BLK, rows), jnp.float32),
                pltpu.VMEM((heads, rows, head_dim), jnp.float32),
                pltpu.VMEM((dev_blocks, BLK, heads, qwidth), queries.dtype),
                pltpu.SemaphoreType.DMA((1,)),
                pltpu.SemaphoreType.DMA((dev_blocks, 5)),
            ],
        ),
        input_output_aliases={6: 0},
    )(rel_start, q2, kv_last, *state, out)
    return out


def solution(mesh):
    placed = (
        P(("grp", "seq"), "head", None),
        P(("grp", "seq"), "head", None),
        P(("grp", "seq"), "head", None),
        P("grp"),
    )

    return jax.shard_map(
        on_device,
        mesh=mesh,
        in_specs=placed,
        out_specs=P(("grp", "seq"), "head", None),
        check_vma=False,
    )
```

```python
import jax
import jax.numpy as jnp
from jax import lax
from jax.experimental import pallas as pl
from jax.experimental.pallas import tpu as pltpu
from jax.sharding import PartitionSpec as P


BLK = 128


def shift_up(block, axis):
    size = lax.axis_size(axis)
    return lax.ppermute(block, axis, [(i, i + 1) for i in range(size - 1)])


def first_needed(distance, reach, dev_blocks):
    return max(0, (distance - reach) * dev_blocks + 1)


def stage_regions(stage, i, dev_blocks, doc_blk, firsts):
    if stage == 0:
        lo, hi = 0, i
    else:
        lo = -stage * dev_blocks + firsts[stage]
        hi = -(stage - 1) * dev_blocks - 1
    lo = max(lo, i - doc_blk + 1)
    rels = list(range(lo, hi + 1))
    regions = []
    while rels:
        take = 2 if len(rels) % 2 == 0 else 1
        regions.append(rels[:take])
        rels = rels[take:]
    return regions


def make_stage(stage, first, last, provisional, dev_blocks, doc_blk, firsts, groups, head_dim, score_scale):
    def local_index(rel):
        if stage == 0:
            return rel
        return rel + stage * dev_blocks - firsts[stage]

    def kernel(rel_ref, q_ref, kv_ref, *refs):
        k_ref = kv_ref.at[0]
        v_ref = kv_ref.at[1]
        if first:
            acc_in = m_in = l_in = None
            rest = refs
        else:
            acc_in, m_in, l_in = refs[:3]
            rest = refs[3:]
        if last:
            o_ref = rest[0]
            (s_sc,) = rest[1:]
        elif provisional:
            acc_out, m_out, l_out, o_ref = rest[:4]
            (s_sc,) = rest[4:]
        else:
            acc_out, m_out, l_out = rest[:3]
            (s_sc,) = rest[3:]

        for i in range(dev_blocks):
            start = rel_ref[i]
            regions = stage_regions(stage, i, dev_blocks, doc_blk, firsts)

            def finish(m_new, row_sum, acc):
                if last or provisional:
                    out = jnp.transpose(acc * (1.0 / row_sum))
                    for g in range(groups):
                        o_ref[i * BLK : (i + 1) * BLK, g * head_dim : (g + 1) * head_dim] = out[
                            g * BLK : (g + 1) * BLK
                        ].astype(o_ref.dtype)
                if not last:
                    acc_out[i] = acc
                    m_out[i : i + 1, :] = m_new
                    l_out[i : i + 1, :] = row_sum

            def passthrough():
                finish(m_in[i : i + 1, :], l_in[i : i + 1, :], acc_in[i])

            if not regions:
                passthrough()
                continue

            def compute():
                q = jnp.concatenate(
                    [q_ref[i * BLK : (i + 1) * BLK, g * head_dim : (g + 1) * head_dim] for g in range(groups)],
                    axis=0,
                )
                m_blk = None
                for r, rels in enumerate(regions):
                    lo = local_index(rels[0])
                    k = k_ref[lo * BLK : (lo + len(rels)) * BLK, :]
                    sc = lax.dot_general(
                        k, q, (((1,), (1,)), ((), ())), preferred_element_type=jnp.float32
                    ) * score_scale
                    key = lax.broadcasted_iota(jnp.int32, sc.shape, 0) // BLK + rels[0]
                    keep = key >= start
                    if rels[-1] == i:
                        key_pos = lax.broadcasted_iota(jnp.int32, sc.shape, 0) + (rels[0] - i) * BLK
                        tok = lax.broadcasted_iota(jnp.int32, sc.shape, 1) % BLK
                        keep = keep & (key_pos <= tok)
                    sc = jnp.where(keep, sc, -jnp.inf)
                    s_sc[r, : len(rels) * BLK, :] = sc
                    mx = jnp.max(sc, axis=0, keepdims=True)
                    m_blk = mx if m_blk is None else jnp.maximum(m_blk, mx)
                if first:
                    m_new = m_blk
                    row_sum = jnp.zeros(m_new.shape, jnp.float32)
                    acc = jnp.zeros((head_dim, groups * BLK), jnp.float32)
                else:
                    m_old = m_in[i : i + 1, :]
                    m_new = jnp.maximum(m_old, m_blk)
                    alpha = jnp.exp(m_old - m_new)
                    row_sum = alpha * l_in[i : i + 1, :]
                    acc = alpha * acc_in[i]
                for r, rels in enumerate(regions):
                    p = jnp.exp(s_sc[r, : len(rels) * BLK, :] - m_new)
                    row_sum = row_sum + jnp.sum(p, axis=0, keepdims=True)
                    lo = local_index(rels[0])
                    v = v_ref[lo * BLK : (lo + len(rels)) * BLK, :]
                    acc = acc + lax.dot_general(
                        v, p.astype(jnp.bfloat16), (((0,), (0,)), ((), ())),
                        preferred_element_type=jnp.float32,
                    )
                finish(m_new, row_sum, acc)

            if first:
                compute()
            else:
                live = start <= regions[-1][-1]
                pl.when(live)(compute)
                pl.when(jnp.logical_not(live))(passthrough)

    return kernel


def make_patch(stage, heads, dev_blocks, doc_blk, firsts, groups, head_dim, score_scale):
    qwidth = groups * head_dim

    def local_index(rel):
        return rel + stage * dev_blocks - firsts[stage]

    def kernel(rel_ref, q_hbm, kv_hbm, acc_hbm, m_hbm, l_hbm, prov_hbm, out_hbm,
               kv_buf, q_buf, acc_buf, m_buf, l_buf, s_sc, o_f32, o_buf, kv_sem, sems):
        del prov_hbm
        blocks = []
        for i in range(dev_blocks):
            regions = stage_regions(stage, i, dev_blocks, doc_blk, firsts)
            if regions:
                blocks.append((i, regions, rel_ref[i] <= regions[-1][-1]))
        if not blocks:
            return
        any_live = blocks[0][2]
        for _, _, live in blocks[1:]:
            any_live = jnp.logical_or(any_live, live)
        kv_copy = pltpu.make_async_copy(kv_hbm, kv_buf, kv_sem.at[0])

        def block_copies(i):
            return [
                pltpu.make_async_copy(q_hbm.at[pl.ds(i * BLK, BLK)], q_buf.at[i], sems.at[i, 0]),
                pltpu.make_async_copy(acc_hbm.at[:, i], acc_buf.at[i], sems.at[i, 1]),
                pltpu.make_async_copy(m_hbm.at[:, pl.ds(i, 1)], m_buf.at[i], sems.at[i, 2]),
                pltpu.make_async_copy(l_hbm.at[:, pl.ds(i, 1)], l_buf.at[i], sems.at[i, 3]),
            ]

        def out_copy(i):
            return pltpu.make_async_copy(o_buf.at[i], out_hbm.at[pl.ds(i * BLK, BLK)], sems.at[i, 4])

        pl.when(any_live)(kv_copy.start)
        for i, _, live in blocks:
            @pl.when(live)
            def _():
                for c in block_copies(i):
                    c.start()
        pl.when(any_live)(kv_copy.wait)

        for i, regions, live in blocks:
            start = rel_ref[i]

            def patch_block():
                for c in block_copies(i):
                    c.wait()
                for h in range(heads):
                    q = jnp.concatenate(
                        [q_buf[i, :, h * qwidth + g * head_dim : h * qwidth + (g + 1) * head_dim] for g in range(groups)],
                        axis=0,
                    )
                    m_blk = None
                    for r, rels in enumerate(regions):
                        lo = local_index(rels[0])
                        k = kv_buf[0, lo * BLK : (lo + len(rels)) * BLK, h * head_dim : (h + 1) * head_dim]
                        sc = lax.dot_general(
                            k, q, (((1,), (1,)), ((), ())), preferred_element_type=jnp.float32
                        ) * score_scale
                        key = lax.broadcasted_iota(jnp.int32, sc.shape, 0) // BLK + rels[0]
                        sc = jnp.where(key >= start, sc, -jnp.inf)
                        s_sc[r, : len(rels) * BLK, :] = sc
                        mx = jnp.max(sc, axis=0, keepdims=True)
                        m_blk = mx if m_blk is None else jnp.maximum(m_blk, mx)
                    m_old = m_buf[i, h]
                    m_new = jnp.maximum(m_old, m_blk)
                    alpha = jnp.exp(m_old - m_new)
                    row_sum = alpha * l_buf[i, h]
                    acc = alpha * acc_buf[i, h]
                    for r, rels in enumerate(regions):
                        p = jnp.exp(s_sc[r, : len(rels) * BLK, :] - m_new)
                        row_sum = row_sum + jnp.sum(p, axis=0, keepdims=True)
                        lo = local_index(rels[0])
                        v = kv_buf[1, lo * BLK : (lo + len(rels)) * BLK, h * head_dim : (h + 1) * head_dim]
                        acc = acc + lax.dot_general(
                            v, p.astype(jnp.bfloat16), (((0,), (0,)), ((), ())),
                            preferred_element_type=jnp.float32,
                        )
                    o_f32[h] = jnp.transpose(acc * (1.0 / row_sum))
                for g in range(groups):
                    vals = jnp.stack([o_f32[h, g * BLK : (g + 1) * BLK, :] for h in range(heads)], axis=1)
                    o_buf[i, :, :, g * head_dim : (g + 1) * head_dim] = vals.astype(o_buf.dtype)
                out_copy(i).start()

            pl.when(live)(patch_block)

        for i, _, live in blocks:
            pl.when(live)(out_copy(i).wait)

    return kernel


def doc_start_of(doc_blocks, blocks):
    ends = jnp.cumsum(doc_blocks)
    starts = ends - doc_blocks
    return jnp.max(jnp.where(starts[None, :] <= blocks[:, None], starts[None, :], 0), axis=1)


def on_device(queries, keys, values, doc_blocks):
    tok_rows, heads, qwidth = queries.shape
    head_dim = keys.shape[2]
    groups = qwidth // head_dim
    rows = groups * BLK
    dev_blocks = tok_rows // BLK
    score_scale = head_dim ** (-0.5)
    reach = min(4, lax.axis_size("seq") // 2)
    doc_blk = reach * dev_blocks
    firsts = [0] + [first_needed(r, reach, dev_blocks) for r in range(1, reach + 1)]

    device_pos = lax.axis_index("seq")
    first_block = device_pos * dev_blocks
    q_blocks = first_block + jnp.arange(dev_blocks, dtype=jnp.int32)
    rel_start = (doc_start_of(doc_blocks, q_blocks) - first_block).astype(jnp.int32)

    q2 = queries.reshape(tok_rows, heads * qwidth)
    k2 = keys.reshape(tok_rows, heads * head_dim)
    v2 = values.reshape(tok_rows, heads * head_dim)

    kv_src = [jnp.stack([k2, v2])]
    k_cur, v_cur = keys, values
    prev_first = 0
    for r in range(1, reach + 1):
        cut = (firsts[r] - prev_first) * BLK
        k_cur, v_cur = shift_up((k_cur[cut:], v_cur[cut:]), "seq")
        prev_first = firsts[r]
        n = k_cur.shape[0]
        kv_src.append(jnp.stack([k_cur.reshape(n, heads * head_dim), v_cur.reshape(n, heads * head_dim)]))

    state_shapes = (
        jax.ShapeDtypeStruct((heads, dev_blocks, head_dim, rows), jnp.float32),
        jax.ShapeDtypeStruct((heads, dev_blocks, rows), jnp.float32),
        jax.ShapeDtypeStruct((heads, dev_blocks, rows), jnp.float32),
    )
    state_specs = [
        pl.BlockSpec((None, dev_blocks, head_dim, rows), lambda h, rel: (h, 0, 0, 0)),
        pl.BlockSpec((None, dev_blocks, rows), lambda h, rel: (h, 0, 0)),
        pl.BlockSpec((None, dev_blocks, rows), lambda h, rel: (h, 0, 0)),
    ]
    scratch = [
        pltpu.VMEM((max(1, (dev_blocks + 1) // 2), 2 * BLK, rows), jnp.float32),
    ]
    q_spec = pl.BlockSpec((tok_rows, qwidth), lambda h, rel: (0, h))

    state = None
    out = None
    for stage in range(reach):
        first = stage == 0
        last = False
        provisional = stage == reach - 1
        kernel = make_stage(stage, first, last, provisional, dev_blocks, doc_blk, firsts, groups, head_dim, score_scale)
        kv_spec = pl.BlockSpec((2, kv_src[stage].shape[1], head_dim), lambda h, rel: (0, 0, h))
        in_specs = [q_spec, kv_spec] + ([] if first else state_specs)
        args = [rel_start, q2, kv_src[stage]] + ([] if first else list(state))
        out_shape = state_shapes
        out_specs = state_specs
        if provisional:
            out_shape = state_shapes + (jax.ShapeDtypeStruct((tok_rows, heads * qwidth), queries.dtype),)
            out_specs = state_specs + [q_spec]
        res = pl.pallas_call(
            kernel,
            out_shape=out_shape,
            grid_spec=pltpu.PrefetchScalarGridSpec(
                num_scalar_prefetch=1,
                grid=(heads,),
                in_specs=in_specs,
                out_specs=out_specs,
                scratch_shapes=scratch,
            ),
            compiler_params=pltpu.CompilerParams(dimension_semantics=("arbitrary",)),
        )(*args)
        state = res[:3]
        if provisional:
            out = res[3].reshape(tok_rows, heads, qwidth)

    n_regions = max(1, (dev_blocks + 1) // 2)
    any_spec = pl.BlockSpec(memory_space=pl.ANY)
    kv_last = kv_src[reach]
    out = pl.pallas_call(
        make_patch(reach, heads, dev_blocks, doc_blk, firsts, groups, head_dim, score_scale),
        out_shape=jax.ShapeDtypeStruct((tok_rows, heads, qwidth), queries.dtype),
        grid_spec=pltpu.PrefetchScalarGridSpec(
            num_scalar_prefetch=1,
            grid=(1,),
            in_specs=[
                any_spec,
                any_spec,
                any_spec,
                any_spec,
                any_spec,
                any_spec,
            ],
            out_specs=any_spec,
            scratch_shapes=[
                pltpu.VMEM(kv_last.shape, kv_last.dtype),
                pltpu.VMEM((dev_blocks, BLK, heads * qwidth), queries.dtype),
                pltpu.VMEM((dev_blocks, heads, head_dim, rows), jnp.float32),
                pltpu.VMEM((dev_blocks, heads, 1, rows), jnp.float32),
                pltpu.VMEM((dev_blocks, heads, 1, rows), jnp.float32),
                pltpu.VMEM((n_regions, 2 * BLK, rows), jnp.float32),
                pltpu.VMEM((heads, rows, head_dim), jnp.float32),
                pltpu.VMEM((dev_blocks, BLK, heads, qwidth), queries.dtype),
                pltpu.SemaphoreType.DMA((1,)),
                pltpu.SemaphoreType.DMA((dev_blocks, 5)),
            ],
        ),
        input_output_aliases={6: 0},
    )(rel_start, q2, kv_last, *state, out)
    return out


def solution(mesh):
    placed = (
        P(("grp", "seq"), "head", None),
        P(("grp", "seq"), "head", None),
        P(("grp", "seq"), "head", None),
        P("grp"),
    )

    return jax.shard_map(
        on_device,
        mesh=mesh,
        in_specs=placed,
        out_specs=P(("grp", "seq"), "head", None),
        check_vma=False,
    )
```

```python
import jax
import jax.numpy as jnp
from jax import lax
from jax.experimental import pallas as pl
from jax.experimental.pallas import tpu as pltpu
from jax.sharding import PartitionSpec as P


BLK = 128


def shift_up(block, axis):
    size = lax.axis_size(axis)
    return lax.ppermute(block, axis, [(i, i + 1) for i in range(size - 1)])


def first_needed(distance, reach, dev_blocks):
    return max(0, (distance - reach) * dev_blocks + 1)


def stage_regions(stage, i, dev_blocks, doc_blk, firsts):
    if stage == 0:
        lo, hi = 0, i
    else:
        lo = -stage * dev_blocks + firsts[stage]
        hi = -(stage - 1) * dev_blocks - 1
    lo = max(lo, i - doc_blk + 1)
    rels = list(range(lo, hi + 1))
    regions = []
    while rels:
        take = 2 if len(rels) % 2 == 0 else 1
        regions.append(rels[:take])
        rels = rels[take:]
    return regions


def make_stage(stage, first, last, provisional, dev_blocks, doc_blk, firsts, groups, head_dim, score_scale):
    def local_index(rel):
        if stage == 0:
            return rel
        return rel + stage * dev_blocks - firsts[stage]

    def kernel(rel_ref, q_ref, kv_ref, *refs):
        k_ref = kv_ref.at[0]
        v_ref = kv_ref.at[1]
        if first:
            acc_in = m_in = l_in = None
            rest = refs
        else:
            acc_in, m_in, l_in = refs[:3]
            rest = refs[3:]
        if last:
            o_ref = rest[0]
            (s_sc,) = rest[1:]
        elif provisional:
            acc_out, m_out, l_out, o_ref = rest[:4]
            (s_sc,) = rest[4:]
        else:
            acc_out, m_out, l_out = rest[:3]
            (s_sc,) = rest[3:]

        for i in range(dev_blocks):
            start = rel_ref[i]
            regions = stage_regions(stage, i, dev_blocks, doc_blk, firsts)

            def finish(m_new, row_sum, acc):
                if last or provisional:
                    out = jnp.transpose(acc * (1.0 / row_sum))
                    for g in range(groups):
                        o_ref[i * BLK : (i + 1) * BLK, g * head_dim : (g + 1) * head_dim] = out[
                            g * BLK : (g + 1) * BLK
                        ].astype(o_ref.dtype)
                if not last:
                    acc_out[i] = acc
                    m_out[i : i + 1, :] = m_new
                    l_out[i : i + 1, :] = row_sum

            def passthrough():
                finish(m_in[i : i + 1, :], l_in[i : i + 1, :], acc_in[i])

            if not regions:
                passthrough()
                continue

            def compute():
                q = jnp.concatenate(
                    [q_ref[i * BLK : (i + 1) * BLK, g * head_dim : (g + 1) * head_dim] for g in range(groups)],
                    axis=0,
                )
                m_blk = None
                for r, rels in enumerate(regions):
                    lo = local_index(rels[0])
                    k = k_ref[lo * BLK : (lo + len(rels)) * BLK, :]
                    sc = lax.dot_general(
                        k, q, (((1,), (1,)), ((), ())), preferred_element_type=jnp.float32
                    ) * score_scale
                    key = lax.broadcasted_iota(jnp.int32, sc.shape, 0) // BLK + rels[0]
                    keep = key >= start
                    if rels[-1] == i:
                        key_pos = lax.broadcasted_iota(jnp.int32, sc.shape, 0) + (rels[0] - i) * BLK
                        tok = lax.broadcasted_iota(jnp.int32, sc.shape, 1) % BLK
                        keep = keep & (key_pos <= tok)
                    sc = jnp.where(keep, sc, -jnp.inf)
                    s_sc[r, : len(rels) * BLK, :] = sc
                    mx = jnp.max(sc, axis=0, keepdims=True)
                    m_blk = mx if m_blk is None else jnp.maximum(m_blk, mx)
                if first:
                    m_new = m_blk
                    row_sum = jnp.zeros(m_new.shape, jnp.float32)
                    acc = jnp.zeros((head_dim, groups * BLK), jnp.float32)
                else:
                    m_old = m_in[i : i + 1, :]
                    m_new = jnp.maximum(m_old, m_blk)
                    alpha = jnp.exp(m_old - m_new)
                    row_sum = alpha * l_in[i : i + 1, :]
                    acc = alpha * acc_in[i]
                for r, rels in enumerate(regions):
                    p = jnp.exp(s_sc[r, : len(rels) * BLK, :] - m_new)
                    row_sum = row_sum + jnp.sum(p, axis=0, keepdims=True)
                    lo = local_index(rels[0])
                    v = v_ref[lo * BLK : (lo + len(rels)) * BLK, :]
                    acc = acc + lax.dot_general(
                        v, p.astype(jnp.bfloat16), (((0,), (0,)), ((), ())),
                        preferred_element_type=jnp.float32,
                    )
                finish(m_new, row_sum, acc)

            if first:
                compute()
            else:
                live = start <= regions[-1][-1]
                pl.when(live)(compute)
                pl.when(jnp.logical_not(live))(passthrough)

    return kernel


def make_patch(stage, heads, dev_blocks, doc_blk, firsts, groups, head_dim, score_scale):
    qwidth = groups * head_dim

    def local_index(rel):
        return rel + stage * dev_blocks - firsts[stage]

    def kernel(rel_ref, q_hbm, kv_hbm, acc_hbm, m_hbm, l_hbm, prov_hbm, out_hbm,
               kv_buf, q_buf, acc_buf, m_buf, l_buf, s_sc, o_f32, o_buf, kv_sem, sems):
        del prov_hbm
        blocks = []
        for i in range(dev_blocks):
            regions = stage_regions(stage, i, dev_blocks, doc_blk, firsts)
            if regions:
                blocks.append((i, regions, rel_ref[i] <= regions[-1][-1]))
        if not blocks:
            return
        any_live = blocks[0][2]
        for _, _, live in blocks[1:]:
            any_live = jnp.logical_or(any_live, live)
        kv_copy = pltpu.make_async_copy(kv_hbm, kv_buf, kv_sem.at[0])

        def block_copies(i):
            return [
                pltpu.make_async_copy(q_hbm.at[pl.ds(i * BLK, BLK)], q_buf.at[i], sems.at[i, 0]),
                pltpu.make_async_copy(acc_hbm.at[:, i], acc_buf.at[i], sems.at[i, 1]),
                pltpu.make_async_copy(m_hbm.at[:, pl.ds(i, 1)], m_buf.at[i], sems.at[i, 2]),
                pltpu.make_async_copy(l_hbm.at[:, pl.ds(i, 1)], l_buf.at[i], sems.at[i, 3]),
            ]

        def out_copy(i):
            return pltpu.make_async_copy(o_buf.at[i], out_hbm.at[pl.ds(i * BLK, BLK)], sems.at[i, 4])

        pl.when(any_live)(kv_copy.start)
        for i, _, live in blocks:
            @pl.when(live)
            def _():
                for c in block_copies(i):
                    c.start()
        pl.when(any_live)(kv_copy.wait)

        for i, regions, live in blocks:
            start = rel_ref[i]

            def patch_block():
                for c in block_copies(i):
                    c.wait()
                for h in range(heads):
                    q = jnp.concatenate(
                        [q_buf[i, :, h * qwidth + g * head_dim : h * qwidth + (g + 1) * head_dim] for g in range(groups)],
                        axis=0,
                    )
                    m_blk = None
                    for r, rels in enumerate(regions):
                        lo = local_index(rels[0])
                        k = kv_buf[0, lo * BLK : (lo + len(rels)) * BLK, h * head_dim : (h + 1) * head_dim]
                        sc = lax.dot_general(
                            k, q, (((1,), (1,)), ((), ())), preferred_element_type=jnp.float32
                        ) * score_scale
                        key = lax.broadcasted_iota(jnp.int32, sc.shape, 0) // BLK + rels[0]
                        sc = jnp.where(key >= start, sc, -jnp.inf)
                        s_sc[r, : len(rels) * BLK, :] = sc
                        mx = jnp.max(sc, axis=0, keepdims=True)
                        m_blk = mx if m_blk is None else jnp.maximum(m_blk, mx)
                    m_old = m_buf[i, h]
                    m_new = jnp.maximum(m_old, m_blk)
                    alpha = jnp.exp(m_old - m_new)
                    row_sum = alpha * l_buf[i, h]
                    acc = alpha * acc_buf[i, h]
                    for r, rels in enumerate(regions):
                        p = jnp.exp(s_sc[r, : len(rels) * BLK, :] - m_new)
                        row_sum = row_sum + jnp.sum(p, axis=0, keepdims=True)
                        lo = local_index(rels[0])
                        v = kv_buf[1, lo * BLK : (lo + len(rels)) * BLK, h * head_dim : (h + 1) * head_dim]
                        acc = acc + lax.dot_general(
                            v, p.astype(jnp.bfloat16), (((0,), (0,)), ((), ())),
                            preferred_element_type=jnp.float32,
                        )
                    o_f32[h] = jnp.transpose(acc * (1.0 / row_sum))
                for g in range(groups):
                    vals = jnp.stack([o_f32[h, g * BLK : (g + 1) * BLK, :] for h in range(heads)], axis=1)
                    o_buf[i, :, :, g * head_dim : (g + 1) * head_dim] = vals.astype(o_buf.dtype)
                out_copy(i).start()

            pl.when(live)(patch_block)

        for i, _, live in blocks:
            pl.when(live)(out_copy(i).wait)

    return kernel


def doc_start_of(doc_blocks, blocks):
    ends = jnp.cumsum(doc_blocks)
    starts = ends - doc_blocks
    return jnp.max(jnp.where(starts[None, :] <= blocks[:, None], starts[None, :], 0), axis=1)


def on_device(queries, keys, values, doc_blocks):
    tok_rows, heads, qwidth = queries.shape
    head_dim = keys.shape[2]
    groups = qwidth // head_dim
    rows = groups * BLK
    dev_blocks = tok_rows // BLK
    score_scale = head_dim ** (-0.5)
    reach = min(4, lax.axis_size("seq") // 2)
    doc_blk = reach * dev_blocks
    firsts = [0] + [first_needed(r, reach, dev_blocks) for r in range(1, reach + 1)]

    device_pos = lax.axis_index("seq")
    first_block = device_pos * dev_blocks
    q_blocks = first_block + jnp.arange(dev_blocks, dtype=jnp.int32)
    rel_start = (doc_start_of(doc_blocks, q_blocks) - first_block).astype(jnp.int32)

    q2 = queries.reshape(tok_rows, heads * qwidth)
    k2 = keys.reshape(tok_rows, heads * head_dim)
    v2 = values.reshape(tok_rows, heads * head_dim)

    kv_src = [jnp.stack([k2, v2])]
    kv_cur = jnp.concatenate([keys, values], axis=1)
    prev_first = 0
    for r in range(1, reach + 1):
        cut = (firsts[r] - prev_first) * BLK
        kv_cur = shift_up(kv_cur[cut:], "seq")
        prev_first = firsts[r]
        n = kv_cur.shape[0]
        kv_src.append(jnp.stack([
            kv_cur[:, :heads].reshape(n, heads * head_dim),
            kv_cur[:, heads:].reshape(n, heads * head_dim),
        ]))

    state_shapes = (
        jax.ShapeDtypeStruct((heads, dev_blocks, head_dim, rows), jnp.float32),
        jax.ShapeDtypeStruct((heads, dev_blocks, rows), jnp.float32),
        jax.ShapeDtypeStruct((heads, dev_blocks, rows), jnp.float32),
    )
    state_specs = [
        pl.BlockSpec((None, dev_blocks, head_dim, rows), lambda h, rel: (h, 0, 0, 0)),
        pl.BlockSpec((None, dev_blocks, rows), lambda h, rel: (h, 0, 0)),
        pl.BlockSpec((None, dev_blocks, rows), lambda h, rel: (h, 0, 0)),
    ]
    scratch = [
        pltpu.VMEM((max(1, (dev_blocks + 1) // 2), 2 * BLK, rows), jnp.float32),
    ]
    q_spec = pl.BlockSpec((tok_rows, qwidth), lambda h, rel: (0, h))

    state = None
    out = None
    for stage in range(reach):
        first = stage == 0
        last = False
        provisional = stage == reach - 1
        kernel = make_stage(stage, first, last, provisional, dev_blocks, doc_blk, firsts, groups, head_dim, score_scale)
        kv_spec = pl.BlockSpec((2, kv_src[stage].shape[1], head_dim), lambda h, rel: (0, 0, h))
        in_specs = [q_spec, kv_spec] + ([] if first else state_specs)
        args = [rel_start, q2, kv_src[stage]] + ([] if first else list(state))
        out_shape = state_shapes
        out_specs = state_specs
        if provisional:
            out_shape = state_shapes + (jax.ShapeDtypeStruct((tok_rows, heads * qwidth), queries.dtype),)
            out_specs = state_specs + [q_spec]
        res = pl.pallas_call(
            kernel,
            out_shape=out_shape,
            grid_spec=pltpu.PrefetchScalarGridSpec(
                num_scalar_prefetch=1,
                grid=(heads,),
                in_specs=in_specs,
                out_specs=out_specs,
                scratch_shapes=scratch,
            ),
            compiler_params=pltpu.CompilerParams(dimension_semantics=("arbitrary",)),
        )(*args)
        state = res[:3]
        if provisional:
            out = res[3].reshape(tok_rows, heads, qwidth)

    n_regions = max(1, (dev_blocks + 1) // 2)
    any_spec = pl.BlockSpec(memory_space=pl.ANY)
    kv_last = kv_src[reach]
    out = pl.pallas_call(
        make_patch(reach, heads, dev_blocks, doc_blk, firsts, groups, head_dim, score_scale),
        out_shape=jax.ShapeDtypeStruct((tok_rows, heads, qwidth), queries.dtype),
        grid_spec=pltpu.PrefetchScalarGridSpec(
            num_scalar_prefetch=1,
            grid=(1,),
            in_specs=[
                any_spec,
                any_spec,
                any_spec,
                any_spec,
                any_spec,
                any_spec,
            ],
            out_specs=any_spec,
            scratch_shapes=[
                pltpu.VMEM(kv_last.shape, kv_last.dtype),
                pltpu.VMEM((dev_blocks, BLK, heads * qwidth), queries.dtype),
                pltpu.VMEM((dev_blocks, heads, head_dim, rows), jnp.float32),
                pltpu.VMEM((dev_blocks, heads, 1, rows), jnp.float32),
                pltpu.VMEM((dev_blocks, heads, 1, rows), jnp.float32),
                pltpu.VMEM((n_regions, 2 * BLK, rows), jnp.float32),
                pltpu.VMEM((heads, rows, head_dim), jnp.float32),
                pltpu.VMEM((dev_blocks, BLK, heads, qwidth), queries.dtype),
                pltpu.SemaphoreType.DMA((1,)),
                pltpu.SemaphoreType.DMA((dev_blocks, 5)),
            ],
        ),
        input_output_aliases={6: 0},
    )(rel_start, q2, kv_last, *state, out)
    return out


def solution(mesh):
    placed = (
        P(("grp", "seq"), "head", None),
        P(("grp", "seq"), "head", None),
        P(("grp", "seq"), "head", None),
        P("grp"),
    )

    return jax.shard_map(
        on_device,
        mesh=mesh,
        in_specs=placed,
        out_specs=P(("grp", "seq"), "head", None),
        check_vma=False,
    )
```

```python
import jax
import jax.numpy as jnp
from jax import lax
from jax.experimental import pallas as pl
from jax.experimental.pallas import tpu as pltpu
from jax.sharding import PartitionSpec as P


BLK = 128


def shift_up(block, axis):
    size = lax.axis_size(axis)
    return lax.ppermute(block, axis, [(i, i + 1) for i in range(size - 1)])


def first_needed(distance, reach, dev_blocks):
    return max(0, (distance - reach) * dev_blocks + 1)


def stage_regions(stage, i, dev_blocks, doc_blk, firsts):
    if stage == 0:
        lo, hi = 0, i
    else:
        lo = -stage * dev_blocks + firsts[stage]
        hi = -(stage - 1) * dev_blocks - 1
    lo = max(lo, i - doc_blk + 1)
    rels = list(range(lo, hi + 1))
    regions = []
    while rels:
        take = 2 if len(rels) % 2 == 0 else 1
        regions.append(rels[:take])
        rels = rels[take:]
    return regions


def make_stage(stage, first, last, provisional, blocked, dev_blocks, doc_blk, firsts, groups, head_dim, score_scale):
    def local_index(rel):
        if stage == 0:
            return rel
        return rel + stage * dev_blocks - firsts[stage]

    def kernel(rel_ref, q_ref, kv_ref, *refs):
        k_ref = kv_ref.at[0]
        v_ref = kv_ref.at[1]
        if first:
            acc_in = m_in = l_in = None
            rest = refs
        else:
            acc_in, m_in, l_in = refs[:3]
            rest = refs[3:]
        if last:
            o_ref = rest[0]
            (s_sc,) = rest[1:]
        elif provisional:
            acc_out, m_out, l_out, o_ref = rest[:4]
            (s_sc,) = rest[4:]
        else:
            acc_out, m_out, l_out = rest[:3]
            (s_sc,) = rest[3:]

        steps = [(pl.program_id(1), 0)] if blocked else [(i, i) for i in range(dev_blocks)]
        for i, qb in steps:
            start = rel_ref[i]
            regions = stage_regions(stage, qb, dev_blocks, doc_blk, firsts)

            def finish(m_new, row_sum, acc):
                if last or provisional:
                    out = jnp.transpose(acc * (1.0 / row_sum))
                    for g in range(groups):
                        o_ref[qb * BLK : (qb + 1) * BLK, g * head_dim : (g + 1) * head_dim] = out[
                            g * BLK : (g + 1) * BLK
                        ].astype(o_ref.dtype)
                if not last:
                    if blocked:
                        acc_out[...] = acc
                    else:
                        acc_out[i] = acc
                    m_out[pl.ds(i, 1), :] = m_new
                    l_out[pl.ds(i, 1), :] = row_sum

            def acc_old():
                return acc_in[...] if blocked else acc_in[i]

            def passthrough():
                finish(m_in[pl.ds(i, 1), :], l_in[pl.ds(i, 1), :], acc_old())

            if not regions:
                passthrough()
                continue

            def compute():
                q = jnp.concatenate(
                    [q_ref[qb * BLK : (qb + 1) * BLK, g * head_dim : (g + 1) * head_dim] for g in range(groups)],
                    axis=0,
                )
                m_blk = None
                for r, rels in enumerate(regions):
                    lo = local_index(rels[0])
                    k = k_ref[lo * BLK : (lo + len(rels)) * BLK, :]
                    sc = lax.dot_general(
                        k, q, (((1,), (1,)), ((), ())), preferred_element_type=jnp.float32
                    ) * score_scale
                    key = lax.broadcasted_iota(jnp.int32, sc.shape, 0) // BLK + rels[0]
                    keep = key >= start
                    if stage == 0 and rels[-1] == qb:
                        key_pos = lax.broadcasted_iota(jnp.int32, sc.shape, 0) + (rels[0] - i) * BLK
                        tok = lax.broadcasted_iota(jnp.int32, sc.shape, 1) % BLK
                        keep = keep & (key_pos <= tok)
                    sc = jnp.where(keep, sc, -jnp.inf)
                    s_sc[r, : len(rels) * BLK, :] = sc
                    mx = jnp.max(sc, axis=0, keepdims=True)
                    m_blk = mx if m_blk is None else jnp.maximum(m_blk, mx)
                if first:
                    m_new = m_blk
                    row_sum = jnp.zeros(m_new.shape, jnp.float32)
                    acc = jnp.zeros((head_dim, groups * BLK), jnp.float32)
                else:
                    m_old = m_in[pl.ds(i, 1), :]
                    m_new = jnp.maximum(m_old, m_blk)
                    alpha = jnp.exp(m_old - m_new)
                    row_sum = alpha * l_in[pl.ds(i, 1), :]
                    acc = alpha * acc_old()
                for r, rels in enumerate(regions):
                    p = jnp.exp(s_sc[r, : len(rels) * BLK, :] - m_new)
                    row_sum = row_sum + jnp.sum(p, axis=0, keepdims=True)
                    lo = local_index(rels[0])
                    v = v_ref[lo * BLK : (lo + len(rels)) * BLK, :]
                    acc = acc + lax.dot_general(
                        v, p.astype(jnp.bfloat16), (((0,), (0,)), ((), ())),
                        preferred_element_type=jnp.float32,
                    )
                finish(m_new, row_sum, acc)

            if first:
                compute()
            else:
                live = start <= regions[-1][-1]
                pl.when(live)(compute)
                pl.when(jnp.logical_not(live))(passthrough)

    return kernel


def make_patch(stage, heads, dev_blocks, doc_blk, firsts, groups, head_dim, score_scale):
    qwidth = groups * head_dim

    def local_index(rel):
        return rel + stage * dev_blocks - firsts[stage]

    def kernel(rel_ref, q_hbm, kv_hbm, acc_hbm, m_hbm, l_hbm, prov_hbm, out_hbm,
               kv_buf, q_buf, acc_buf, m_buf, l_buf, s_sc, o_f32, o_buf, kv_sem, sems):
        del prov_hbm
        blocks = []
        for i in range(dev_blocks):
            regions = stage_regions(stage, i, dev_blocks, doc_blk, firsts)
            if regions:
                blocks.append((i, regions, rel_ref[i] <= regions[-1][-1]))
        if not blocks:
            return
        any_live = blocks[0][2]
        for _, _, live in blocks[1:]:
            any_live = jnp.logical_or(any_live, live)
        kv_copy = pltpu.make_async_copy(kv_hbm, kv_buf, kv_sem.at[0])

        def block_copies(i):
            return [
                pltpu.make_async_copy(q_hbm.at[pl.ds(i * BLK, BLK)], q_buf.at[i], sems.at[i, 0]),
                pltpu.make_async_copy(acc_hbm.at[:, i], acc_buf.at[i], sems.at[i, 1]),
                pltpu.make_async_copy(m_hbm.at[:, pl.ds(i, 1)], m_buf.at[i], sems.at[i, 2]),
                pltpu.make_async_copy(l_hbm.at[:, pl.ds(i, 1)], l_buf.at[i], sems.at[i, 3]),
            ]

        def out_copy(i):
            return pltpu.make_async_copy(o_buf.at[i], out_hbm.at[pl.ds(i * BLK, BLK)], sems.at[i, 4])

        pl.when(any_live)(kv_copy.start)
        for i, _, live in blocks:
            @pl.when(live)
            def _():
                for c in block_copies(i):
                    c.start()
        pl.when(any_live)(kv_copy.wait)

        for i, regions, live in blocks:
            start = rel_ref[i]

            def patch_block():
                for c in block_copies(i):
                    c.wait()
                for h in range(heads):
                    q = jnp.concatenate(
                        [q_buf[i, :, h * qwidth + g * head_dim : h * qwidth + (g + 1) * head_dim] for g in range(groups)],
                        axis=0,
                    )
                    m_blk = None
                    for r, rels in enumerate(regions):
                        lo = local_index(rels[0])
                        k = kv_buf[0, lo * BLK : (lo + len(rels)) * BLK, h * head_dim : (h + 1) * head_dim]
                        sc = lax.dot_general(
                            k, q, (((1,), (1,)), ((), ())), preferred_element_type=jnp.float32
                        ) * score_scale
                        key = lax.broadcasted_iota(jnp.int32, sc.shape, 0) // BLK + rels[0]
                        sc = jnp.where(key >= start, sc, -jnp.inf)
                        s_sc[r, : len(rels) * BLK, :] = sc
                        mx = jnp.max(sc, axis=0, keepdims=True)
                        m_blk = mx if m_blk is None else jnp.maximum(m_blk, mx)
                    m_old = m_buf[i, h]
                    m_new = jnp.maximum(m_old, m_blk)
                    alpha = jnp.exp(m_old - m_new)
                    row_sum = alpha * l_buf[i, h]
                    acc = alpha * acc_buf[i, h]
                    for r, rels in enumerate(regions):
                        p = jnp.exp(s_sc[r, : len(rels) * BLK, :] - m_new)
                        row_sum = row_sum + jnp.sum(p, axis=0, keepdims=True)
                        lo = local_index(rels[0])
                        v = kv_buf[1, lo * BLK : (lo + len(rels)) * BLK, h * head_dim : (h + 1) * head_dim]
                        acc = acc + lax.dot_general(
                            v, p.astype(jnp.bfloat16), (((0,), (0,)), ((), ())),
                            preferred_element_type=jnp.float32,
                        )
                    o_f32[h] = jnp.transpose(acc * (1.0 / row_sum))
                for g in range(groups):
                    vals = jnp.stack([o_f32[h, g * BLK : (g + 1) * BLK, :] for h in range(heads)], axis=1)
                    o_buf[i, :, :, g * head_dim : (g + 1) * head_dim] = vals.astype(o_buf.dtype)
                out_copy(i).start()

            pl.when(live)(patch_block)

        for i, _, live in blocks:
            pl.when(live)(out_copy(i).wait)

    return kernel


def doc_start_of(doc_blocks, blocks):
    ends = jnp.cumsum(doc_blocks)
    starts = ends - doc_blocks
    return jnp.max(jnp.where(starts[None, :] <= blocks[:, None], starts[None, :], 0), axis=1)


def on_device(queries, keys, values, doc_blocks):
    tok_rows, heads, qwidth = queries.shape
    head_dim = keys.shape[2]
    groups = qwidth // head_dim
    rows = groups * BLK
    dev_blocks = tok_rows // BLK
    score_scale = head_dim ** (-0.5)
    reach = min(4, lax.axis_size("seq") // 2)
    doc_blk = reach * dev_blocks
    firsts = [0] + [first_needed(r, reach, dev_blocks) for r in range(1, reach + 1)]

    device_pos = lax.axis_index("seq")
    first_block = device_pos * dev_blocks
    q_blocks = first_block + jnp.arange(dev_blocks, dtype=jnp.int32)
    rel_start = (doc_start_of(doc_blocks, q_blocks) - first_block).astype(jnp.int32)

    q2 = queries.reshape(tok_rows, heads * qwidth)
    k2 = keys.reshape(tok_rows, heads * head_dim)
    v2 = values.reshape(tok_rows, heads * head_dim)

    kv_cur = jnp.stack([k2, v2])
    kv_src = [kv_cur]
    prev_first = 0
    for r in range(1, reach + 1):
        cut = (firsts[r] - prev_first) * BLK
        kv_cur = shift_up(kv_cur[:, cut:], "seq")
        prev_first = firsts[r]
        kv_src.append(kv_cur)

    state_shapes = (
        jax.ShapeDtypeStruct((heads, dev_blocks, head_dim, rows), jnp.float32),
        jax.ShapeDtypeStruct((heads, dev_blocks, rows), jnp.float32),
        jax.ShapeDtypeStruct((heads, dev_blocks, rows), jnp.float32),
    )
    state_specs = [
        pl.BlockSpec((None, dev_blocks, head_dim, rows), lambda h, rel: (h, 0, 0, 0)),
        pl.BlockSpec((None, dev_blocks, rows), lambda h, rel: (h, 0, 0)),
        pl.BlockSpec((None, dev_blocks, rows), lambda h, rel: (h, 0, 0)),
    ]
    scratch = [
        pltpu.VMEM((max(1, (dev_blocks + 1) // 2), 2 * BLK, rows), jnp.float32),
    ]
    q_spec = pl.BlockSpec((tok_rows, qwidth), lambda h, rel: (0, h))

    state = None
    out = None
    for stage in range(reach):
        first = stage == 0
        last = False
        provisional = stage == reach - 1
        blocked = not first and all(
            stage_regions(stage, i, dev_blocks, doc_blk, firsts) == stage_regions(stage, 0, dev_blocks, doc_blk, firsts)
            for i in range(dev_blocks)
        )
        kernel = make_stage(stage, first, last, provisional, blocked, dev_blocks, doc_blk, firsts, groups, head_dim, score_scale)
        if blocked:
            grid = (heads, dev_blocks)
            q_sp = pl.BlockSpec((BLK, qwidth), lambda h, i, rel: (i, h))
            kv_spec = pl.BlockSpec((2, kv_src[stage].shape[1], head_dim), lambda h, i, rel: (0, 0, h))
            st_specs = [
                pl.BlockSpec((None, None, head_dim, rows), lambda h, i, rel: (h, i, 0, 0)),
                pl.BlockSpec((None, dev_blocks, rows), lambda h, i, rel: (h, 0, 0)),
                pl.BlockSpec((None, dev_blocks, rows), lambda h, i, rel: (h, 0, 0)),
            ]
            sem = ("arbitrary", "arbitrary")
        else:
            grid = (heads,)
            q_sp = q_spec
            kv_spec = pl.BlockSpec((2, kv_src[stage].shape[1], head_dim), lambda h, rel: (0, 0, h))
            st_specs = state_specs
            sem = ("arbitrary",)
        in_specs = [q_sp, kv_spec] + ([] if first else st_specs)
        args = [rel_start, q2, kv_src[stage]] + ([] if first else list(state))
        out_shape = state_shapes
        out_specs = st_specs
        if provisional:
            out_shape = state_shapes + (jax.ShapeDtypeStruct((tok_rows, heads * qwidth), queries.dtype),)
            out_specs = st_specs + [q_sp]
        res = pl.pallas_call(
            kernel,
            out_shape=out_shape,
            grid_spec=pltpu.PrefetchScalarGridSpec(
                num_scalar_prefetch=1,
                grid=grid,
                in_specs=in_specs,
                out_specs=out_specs,
                scratch_shapes=scratch,
            ),
            compiler_params=pltpu.CompilerParams(dimension_semantics=sem),
        )(*args)
        state = res[:3]
        if provisional:
            out = res[3].reshape(tok_rows, heads, qwidth)

    n_regions = max(1, (dev_blocks + 1) // 2)
    any_spec = pl.BlockSpec(memory_space=pl.ANY)
    kv_last = kv_src[reach]
    out = pl.pallas_call(
        make_patch(reach, heads, dev_blocks, doc_blk, firsts, groups, head_dim, score_scale),
        out_shape=jax.ShapeDtypeStruct((tok_rows, heads, qwidth), queries.dtype),
        grid_spec=pltpu.PrefetchScalarGridSpec(
            num_scalar_prefetch=1,
            grid=(1,),
            in_specs=[
                any_spec,
                any_spec,
                any_spec,
                any_spec,
                any_spec,
                any_spec,
            ],
            out_specs=any_spec,
            scratch_shapes=[
                pltpu.VMEM(kv_last.shape, kv_last.dtype),
                pltpu.VMEM((dev_blocks, BLK, heads * qwidth), queries.dtype),
                pltpu.VMEM((dev_blocks, heads, head_dim, rows), jnp.float32),
                pltpu.VMEM((dev_blocks, heads, 1, rows), jnp.float32),
                pltpu.VMEM((dev_blocks, heads, 1, rows), jnp.float32),
                pltpu.VMEM((n_regions, 2 * BLK, rows), jnp.float32),
                pltpu.VMEM((heads, rows, head_dim), jnp.float32),
                pltpu.VMEM((dev_blocks, BLK, heads, qwidth), queries.dtype),
                pltpu.SemaphoreType.DMA((1,)),
                pltpu.SemaphoreType.DMA((dev_blocks, 5)),
            ],
        ),
        input_output_aliases={6: 0},
    )(rel_start, q2, kv_last, *state, out)
    return out


def solution(mesh):
    placed = (
        P(("grp", "seq"), "head", None),
        P(("grp", "seq"), "head", None),
        P(("grp", "seq"), "head", None),
        P("grp"),
    )

    return jax.shard_map(
        on_device,
        mesh=mesh,
        in_specs=placed,
        out_specs=P(("grp", "seq"), "head", None),
        check_vma=False,
    )
```
